32 devices in a mesh: lat: 4 (over y, x), lon: 8 (over z, core).
Axes of the slice: x: 2, y: 2, z: 4, core: 2. Of those that a mesh axis runs over, the one named last changes fastest.
Arguments:
- fields: float32 [5, 8, 64, 5760], P(None, None, 'lat', 'lon'), may hold values from -10 to 10
- lon_courant: float32 [8, 64, 5760], P(None, 'lat', 'lon'), may hold values from -0.45 to 0.45
- lat_courant: float32 [8, 64, 5760], P(None, 'lat', 'lon'), may hold values from -0.45 to 0.45
- filter_rows: int32 [32], replicated, may hold values from 0 to 63, as said below
- cutoff: int32 [32], replicated, may hold values from 90 to 1440
Outputs:
- advanced: float32 [5, 8, 64, 5760], P(None, None, 'lat', 'lon')
The draws below stay inside these ranges and needn't reach their ends.
Inputs may be any that keep to these rules, and one draw needn't show every extreme that they name: `filter_rows`: sorted ascending and distinct: the first entries are the rows 0, 1, 2, ... and the rest the rows up to 63, the first group holding between 8 and 24 rows.
All inputs are finite; a program needn't handle non-finite values.
Results may differ from the reference program's by a relative error of at most 0.00005.
Values sent between devices are 32-bit elements; how exact they have to be, the bound alone decides.
No kernel may reach another device: no remote copies, remote signals or barrier semaphores. Data moves between devices by JAX's collectives and lax.ppermute only.
A program may use at most 64 MiB of HBM per device.

```python
import math
import jax
import jax.numpy as jnp
from jax import lax

NLON = 5760
FIELDS = 5
LEV = 8
NLAT = 64
NFILT = 32


def shared_rows(key):
    row_key = jax.random.fold_in(key, 11)
    north_count = jax.random.randint(row_key, (), NFILT // 4, 3 * NFILT // 4 + 1)
    position = jnp.arange(NFILT, dtype=jnp.int32)
    return jnp.where(position < north_count, position, NLAT - NFILT + position).astype(jnp.int32)


def shared_cutoff(key):
    cut_keys = jax.random.split(jax.random.fold_in(key, 23), 5)
    lowest = NLON // 64
    highest = NLON // 4
    polar_class = jax.random.randint(cut_keys[0], (NFILT,), 0, 2)
    near_cut = lowest + jax.random.randint(cut_keys[1], (NFILT,), 0, lowest // 2 + 1)
    wide_cut = jax.random.randint(cut_keys[2], (NFILT,), lowest, highest + 1)
    chosen = jnp.where(polar_class == 1, near_cut, wide_cut)
    low_slot = jax.random.randint(cut_keys[3], (), 0, NFILT)
    high_slot = (low_slot + 1 + jax.random.randint(cut_keys[4], (), 0, NFILT - 1)) % NFILT
    chosen = chosen.at[low_slot].set(lowest).at[high_slot].set(highest)
    return chosen.astype(jnp.int32)


def draw_filter_rows(key, part):
    return shared_rows(key)


def draw_cutoff(key, part):
    return shared_cutoff(key)


def signed_courant(key, lowest_size):
    sign_key, size_key = jax.random.split(key)
    row_sign = (2 * jax.random.randint(sign_key, (LEV, NLAT, 1), 0, 2) - 1).astype(jnp.float32)
    magnitude = jax.random.uniform(size_key, (LEV, NLAT, NLON), jnp.float32, lowest_size, 0.45)
    return row_sign * magnitude


def draw_lon_courant(key, part):
    lowest_size = 0.2
    return signed_courant(jax.random.fold_in(key, 41), lowest_size)


def draw_lat_courant(key, part):
    lowest_size = 0.2
    return signed_courant(jax.random.fold_in(key, 43), lowest_size)


def draw_fields(key, part):
    filtered = shared_rows(key)
    cut_values = shared_cutoff(key)
    wave_keys = jax.random.split(jax.random.fold_in(key, 47), 20)
    row_center = jax.random.randint(wave_keys[0], (NLAT,), NLON // 64, NLON // 4 + 1).astype(jnp.int32)
    row_center = row_center.at[filtered].set(cut_values)
    columns = jnp.arange(NLON, dtype=jnp.int32)
    background = jnp.clip(jax.random.normal(wave_keys[19], (FIELDS, LEV, NLAT, NLON), jnp.float32), -4.0, 4.0)
    total = background
    for packet in range(6):
        if packet < 2:
            offset = jax.random.randint(wave_keys[1 + 3 * packet], (FIELDS, LEV, NLAT), 0, NLON // 144 + 1)
        else:
            offset = jax.random.randint(wave_keys[1 + 3 * packet], (FIELDS, LEV, NLAT), NLON // 88, NLON // 36 + 1)
        flip = 2 * jax.random.randint(wave_keys[2 + 3 * packet], (FIELDS, LEV, NLAT), 0, 2) - 1
        wave_number = jnp.clip(row_center[None, None, :] + flip * offset, 1, NLON // 2 - 1).astype(jnp.int32)
        phase = jax.random.uniform(wave_keys[3 + 3 * packet], (FIELDS, LEV, NLAT, 1), jnp.float32, 0.0, 2.0 * math.pi)
        turn = (wave_number[..., None] * columns % NLON).astype(jnp.float32) * (2.0 * math.pi / NLON)
        total = total + jnp.cos(turn + phase)
    return total.astype(jnp.float32)


def setup_inputs(seed: int = 0) -> dict:
    arg_keys = jax.random.split(jax.random.key(seed), 6)
    return {
        "fields": draw_fields(jax.random.fold_in(arg_keys[5], 71), 0),
        "lon_courant": draw_lon_courant(jax.random.fold_in(arg_keys[5], 71), 0),
        "lat_courant": draw_lat_courant(jax.random.fold_in(arg_keys[5], 71), 0),
        "filter_rows": draw_filter_rows(jax.random.fold_in(arg_keys[5], 71), 0),
        "cutoff": draw_cutoff(jax.random.fold_in(arg_keys[5], 71), 0),
    }


def damping_factor(mode_value, cut_value):
    return jnp.where(mode_value <= cut_value, 1.0, (cut_value / jnp.maximum(mode_value, 1.0)) ** 2)


def level_increment(field_block, lon_courant, lat_courant):
    east_side = jnp.roll(field_block, -1, axis=2)
    east_flux = 0.5 * lon_courant * (field_block + east_side) - 0.5 * lon_courant * lon_courant * (east_side - field_block)
    west_flux = jnp.roll(east_flux, 1, axis=2)
    zero_row = jnp.zeros_like(field_block[:, :1])
    north_side = jnp.concatenate([field_block[:, 1:], zero_row], axis=1)
    north_flux = 0.5 * lat_courant * (field_block + north_side) - 0.5 * lat_courant * lat_courant * (north_side - field_block)
    north_flux = north_flux.at[:, -1].set(0.0)
    south_flux = jnp.concatenate([jnp.zeros_like(north_flux[:, :1]), north_flux[:, :-1]], axis=1)
    return -(east_flux - west_flux) - (north_flux - south_flux)


def smooth_rows(increment_rows, cut_values):
    spectrum = jnp.fft.rfft(increment_rows, axis=-1)
    modes = jnp.arange(NLON // 2 + 1).astype(jnp.float32)
    damp = damping_factor(modes[None, :], cut_values.astype(jnp.float32)[:, None])
    return jnp.fft.irfft(spectrum * damp, n=NLON, axis=-1).astype(increment_rows.dtype)


def reference(fields, lon_courant, lat_courant, filter_rows, cutoff):
    def one_field(field_block):
        increment = level_increment(field_block, lon_courant, lat_courant)
        smoothed = smooth_rows(increment[:, filter_rows], cutoff)
        increment = increment.at[:, filter_rows].set(smoothed)
        return field_block + increment

    return lax.map(one_field, fields)
```

```python
from functools import partial
import math

import jax
import jax.numpy as jnp
from jax import lax
from jax.sharding import PartitionSpec as P

radix_len = 128


def with_halo(x, sides, width, wrap):
    for axis, dim in sides:
        size, length = (lax.axis_size(axis), x.shape[dim])
        up = [(i, (i + 1) % size) for i in range(size if wrap else size - 1)]
        down = [(j, i) for i, j in up]
        last = lax.slice_in_dim(x, length - width, length, axis=dim)
        leading = lax.slice_in_dim(x, 0, width, axis=dim)
        before = lax.ppermute(last, axis, up)
        after = lax.ppermute(leading, axis, down)
        x = jnp.concatenate([before, x, after], axis=dim)
    return x


def phase_table(row_total, col_total, modulus):
    product = (
        jnp.arange(row_total, dtype=jnp.int32)[:, None]
        * jnp.arange(col_total, dtype=jnp.int32)[None, :]
        % modulus
    )
    angle = product.astype(jnp.float32) * (2.0 * math.pi / modulus)
    return (jnp.cos(angle), jnp.sin(angle))


def filter_lines(lines, line_cut):
    line_total, circle = lines.shape
    outer = circle // radix_len
    mixer = partial(jnp.einsum, precision=lax.Precision.HIGHEST)
    outer_cos, outer_sin = phase_table(outer, outer, outer)
    inner_cos, inner_sin = phase_table(radix_len, radix_len, radix_len)
    twist_cos, twist_sin = phase_table(outer, radix_len, circle)
    values = lines.reshape(line_total, outer, radix_len)
    first_re = mixer("lan,aj->ljn", values, outer_cos)
    first_im = -mixer("lan,aj->ljn", values, outer_sin)
    turned_re = first_re * twist_cos + first_im * twist_sin
    turned_im = first_im * twist_cos - first_re * twist_sin
    spec_re = mixer("ljn,nk->ljk", turned_re, inner_cos) + mixer(
        "ljn,nk->ljk", turned_im, inner_sin
    )
    spec_im = mixer("ljn,nk->ljk", turned_im, inner_cos) - mixer(
        "ljn,nk->ljk", turned_re, inner_sin
    )
    wave = (
        jnp.arange(outer, dtype=jnp.int32)[:, None]
        + outer * jnp.arange(radix_len, dtype=jnp.int32)[None, :]
    )
    mode_value = jnp.minimum(wave, circle - wave).astype(jnp.float32)[None]
    cut_value = line_cut[:, None, None]
    damp = jnp.where(mode_value <= cut_value, 1.0, (cut_value / jnp.maximum(mode_value, 1.0)) ** 2)
    spec_re = spec_re * damp
    spec_im = spec_im * damp
    back_re = mixer("ljk,kn->ljn", spec_re, inner_cos) - mixer("ljk,kn->ljn", spec_im, inner_sin)
    back_im = mixer("ljk,kn->ljn", spec_im, inner_cos) + mixer("ljk,kn->ljn", spec_re, inner_sin)
    untwist_re = back_re * twist_cos - back_im * twist_sin
    untwist_im = back_im * twist_cos + back_re * twist_sin
    result = mixer("ljn,ja->lan", untwist_re, outer_cos) - mixer(
        "ljn,ja->lan", untwist_im, outer_sin
    )
    return (result / circle).reshape(line_total, circle)


def face_flux(courant, near_value, far_value):
    return 0.5 * courant * (near_value + far_value) - 0.5 * courant * courant * (
        far_value - near_value
    )


def body(fields, lon_courant, lat_courant, filter_rows, cutoff):
    field_count, level_count, rows_dev, columns = fields.shape
    stacked = field_count * level_count
    lon_devices = lax.axis_size("lon")
    lat_devices = lax.axis_size("lat")
    total_lon = columns * lon_devices
    flat_fields = fields.reshape(stacked, rows_dev, columns)
    east_west = with_halo(
        jnp.concatenate([flat_fields, lon_courant], axis=0), (("lon", 2),), 1, True
    )
    north_south = with_halo(
        jnp.concatenate([flat_fields, lat_courant], axis=0), (("lat", 1),), 1, False
    )
    wide_fields = east_west[:stacked].reshape(field_count, level_count, rows_dev, columns + 2)
    wide_courant = east_west[stacked:]
    column_flux = face_flux(wide_courant[..., :-1], wide_fields[..., :-1], wide_fields[..., 1:])
    tall_fields = north_south[:stacked].reshape(field_count, level_count, rows_dev + 2, columns)
    tall_courant = north_south[stacked:]
    row_flux = face_flux(tall_courant[:, :-1], tall_fields[:, :, :-1], tall_fields[:, :, 1:])
    tile_index = lax.axis_index("lat")
    lower_row = tile_index * rows_dev - 1 + jnp.arange(rows_dev + 1, dtype=jnp.int32)
    row_flux = jnp.where((lower_row == rows_dev * lat_devices - 1)[:, None], 0.0, row_flux)
    increment = -(column_flux[..., 1:] - column_flux[..., :-1]) - (
        row_flux[:, :, 1:] - row_flux[:, :, :-1]
    )
    flat_increment = increment.reshape(stacked, rows_dev, columns)
    half_rows = rows_dev // 2
    pair_shift = lat_devices // 2
    pair_perm = [(i, (i + pair_shift) % lat_devices) for i in range(lat_devices)]
    is_low = tile_index < pair_shift
    partner_index = (tile_index + pair_shift) % lat_devices

    def row_info(tile):
        row_global = tile * rows_dev + jnp.arange(rows_dev, dtype=jnp.int32)
        matched = filter_rows[None, :] == row_global[:, None]
        return jnp.any(matched, axis=1), jnp.sum(jnp.where(matched, cutoff[None, :], 0), axis=1)

    is_filtered, own_cut = row_info(tile_index)
    _, partner_cut = row_info(partner_index)
    row_cut = jnp.where(is_filtered, own_cut, partner_cut).astype(jnp.float32)
    low_half = flat_increment[:, :half_rows]
    high_half = flat_increment[:, half_rows:]
    kept = jnp.where(is_low, low_half, high_half)
    given = jnp.where(is_low, high_half, low_half)
    taken = lax.ppermute(given, "lat", pair_perm)
    kept_filtered = jnp.where(is_low, is_filtered[:half_rows], is_filtered[half_rows:])
    kept_cut = jnp.where(is_low, row_cut[:half_rows], row_cut[half_rows:])
    pair_lines = jnp.where(kept_filtered[None, :, None], kept, taken)
    line_count = stacked * half_rows // lon_devices
    full_lines = lax.all_to_all(
        pair_lines.reshape(stacked * half_rows, columns),
        "lon",
        split_axis=0,
        concat_axis=1,
        tiled=True,
    )
    line_index = lax.axis_index("lon") * line_count + jnp.arange(line_count, dtype=jnp.int32)
    smoothed = filter_lines(full_lines, kept_cut[line_index % half_rows])
    returned = lax.all_to_all(smoothed, "lon", split_axis=1, concat_axis=0, tiled=True).reshape(
        stacked, half_rows, columns
    )
    handed_back = lax.ppermute(returned, "lat", pair_perm)
    smooth_rows = jnp.where(
        is_low,
        jnp.concatenate([returned, handed_back], axis=1),
        jnp.concatenate([handed_back, returned], axis=1),
    )
    final_increment = jnp.where(is_filtered[None, :, None], smooth_rows, flat_increment)
    return (flat_fields + final_increment).reshape(fields.shape)


def solution(mesh):
    placed = (P(None, None, "lat", "lon"), P(None, "lat", "lon"), P(None, "lat", "lon"), P(), P())
    return jax.shard_map(
        body, mesh=mesh, in_specs=placed, out_specs=P(None, None, "lat", "lon"), check_vma=False
    )
```

```python
from functools import partial
import math

import jax
import jax.numpy as jnp
from jax import lax
from jax.sharding import PartitionSpec as P

radix_len = 128


def phase_table(row_total, col_total, modulus):
    product = (
        jnp.arange(row_total, dtype=jnp.int32)[:, None]
        * jnp.arange(col_total, dtype=jnp.int32)[None, :]
        % modulus
    )
    angle = product.astype(jnp.float32) * (2.0 * math.pi / modulus)
    return (jnp.cos(angle), jnp.sin(angle))


def filter_lines(lines, line_cut):
    line_total, circle = lines.shape
    outer = circle // radix_len
    mixer = partial(jnp.einsum, precision=lax.Precision.HIGHEST)
    outer_cos, outer_sin = phase_table(outer, outer, outer)
    inner_cos, inner_sin = phase_table(radix_len, radix_len, radix_len)
    twist_cos, twist_sin = phase_table(outer, radix_len, circle)
    values = lines.reshape(line_total, outer, radix_len)
    first_re = mixer("lan,aj->ljn", values, outer_cos)
    first_im = -mixer("lan,aj->ljn", values, outer_sin)
    turned_re = first_re * twist_cos + first_im * twist_sin
    turned_im = first_im * twist_cos - first_re * twist_sin
    spec_re = mixer("ljn,nk->ljk", turned_re, inner_cos) + mixer(
        "ljn,nk->ljk", turned_im, inner_sin
    )
    spec_im = mixer("ljn,nk->ljk", turned_im, inner_cos) - mixer(
        "ljn,nk->ljk", turned_re, inner_sin
    )
    wave = (
        jnp.arange(outer, dtype=jnp.int32)[:, None]
        + outer * jnp.arange(radix_len, dtype=jnp.int32)[None, :]
    )
    mode_value = jnp.minimum(wave, circle - wave).astype(jnp.float32)[None]
    cut_value = line_cut[:, None, None]
    damp = jnp.where(mode_value <= cut_value, 1.0, (cut_value / jnp.maximum(mode_value, 1.0)) ** 2)
    spec_re = spec_re * damp
    spec_im = spec_im * damp
    back_re = mixer("ljk,kn->ljn", spec_re, inner_cos) - mixer("ljk,kn->ljn", spec_im, inner_sin)
    back_im = mixer("ljk,kn->ljn", spec_im, inner_cos) + mixer("ljk,kn->ljn", spec_re, inner_sin)
    untwist_re = back_re * twist_cos - back_im * twist_sin
    untwist_im = back_im * twist_cos + back_re * twist_sin
    result = mixer("ljn,ja->lan", untwist_re, outer_cos) - mixer(
        "ljn,ja->lan", untwist_im, outer_sin
    )
    return (result / circle).reshape(line_total, circle)


def face_flux(courant, near_value, far_value):
    return 0.5 * courant * (near_value + far_value) - 0.5 * courant * courant * (
        far_value - near_value
    )


def body(fields, lon_courant, lat_courant, filter_rows, cutoff):
    field_count, level_count, rows_dev, columns = fields.shape
    stacked = field_count * level_count
    lon_devices = lax.axis_size("lon")
    lat_devices = lax.axis_size("lat")
    flat_fields = fields.reshape(stacked, rows_dev, columns)
    eastward = [(i, (i + 1) % lon_devices) for i in range(lon_devices)]
    westward = [((i + 1) % lon_devices, i) for i in range(lon_devices)]
    northward = [(i, i + 1) for i in range(lat_devices - 1)]
    southward = [(i + 1, i) for i in range(lat_devices - 1)]
    from_west = lax.ppermute(
        jnp.concatenate([flat_fields[..., -1], lon_courant[..., -1]], axis=0), "lon", eastward
    )
    from_east = lax.ppermute(flat_fields[..., 0], "lon", westward)
    from_below = lax.ppermute(
        jnp.concatenate([flat_fields[:, -1], lat_courant[:, -1]], axis=0), "lat", northward
    )
    from_above = lax.ppermute(flat_fields[:, 0], "lat", southward)
    wide_fields = jnp.concatenate(
        [from_west[:stacked, :, None], flat_fields, from_east[:, :, None]], axis=2
    ).reshape(field_count, level_count, rows_dev, columns + 2)
    wide_courant = jnp.concatenate([from_west[stacked:, :, None], lon_courant], axis=2)
    column_flux = face_flux(wide_courant, wide_fields[..., :-1], wide_fields[..., 1:])
    tall_fields = jnp.concatenate(
        [from_below[:stacked, None], flat_fields, from_above[:, None]], axis=1
    ).reshape(field_count, level_count, rows_dev + 2, columns)
    tall_courant = jnp.concatenate([from_below[stacked:, None], lat_courant], axis=1)
    row_flux = face_flux(tall_courant, tall_fields[:, :, :-1], tall_fields[:, :, 1:])
    tile_index = lax.axis_index("lat")
    lower_row = tile_index * rows_dev - 1 + jnp.arange(rows_dev + 1, dtype=jnp.int32)
    row_flux = jnp.where((lower_row == rows_dev * lat_devices - 1)[:, None], 0.0, row_flux)
    increment = -(column_flux[..., 1:] - column_flux[..., :-1]) - (
        row_flux[:, :, 1:] - row_flux[:, :, :-1]
    )
    flat_increment = increment.reshape(stacked, rows_dev, columns)
    half_rows = rows_dev // 2
    pair_shift = lat_devices // 2
    pair_perm = [(i, (i + pair_shift) % lat_devices) for i in range(lat_devices)]
    is_low = tile_index < pair_shift
    partner_index = (tile_index + pair_shift) % lat_devices

    def row_info(tile):
        row_global = tile * rows_dev + jnp.arange(rows_dev, dtype=jnp.int32)
        matched = filter_rows[None, :] == row_global[:, None]
        return jnp.any(matched, axis=1), jnp.sum(jnp.where(matched, cutoff[None, :], 0), axis=1)

    is_filtered, own_cut = row_info(tile_index)
    _, partner_cut = row_info(partner_index)
    row_cut = jnp.where(is_filtered, own_cut, partner_cut).astype(jnp.float32)
    low_half = flat_increment[:, :half_rows]
    high_half = flat_increment[:, half_rows:]
    kept = jnp.where(is_low, low_half, high_half)
    given = jnp.where(is_low, high_half, low_half)
    taken = lax.ppermute(given, "lat", pair_perm)
    kept_filtered = jnp.where(is_low, is_filtered[:half_rows], is_filtered[half_rows:])
    kept_cut = jnp.where(is_low, row_cut[:half_rows], row_cut[half_rows:])
    pair_lines = jnp.where(kept_filtered[None, :, None], kept, taken)
    line_count = stacked * half_rows // lon_devices
    full_lines = lax.all_to_all(
        pair_lines.reshape(stacked * half_rows, columns),
        "lon",
        split_axis=0,
        concat_axis=1,
        tiled=True,
    )
    line_index = lax.axis_index("lon") * line_count + jnp.arange(line_count, dtype=jnp.int32)
    smoothed = filter_lines(full_lines, kept_cut[line_index % half_rows])
    returned = lax.all_to_all(smoothed, "lon", split_axis=1, concat_axis=0, tiled=True).reshape(
        stacked, half_rows, columns
    )
    handed_back = lax.ppermute(returned, "lat", pair_perm)
    smooth_rows = jnp.where(
        is_low,
        jnp.concatenate([returned, handed_back], axis=1),
        jnp.concatenate([handed_back, returned], axis=1),
    )
    final_increment = jnp.where(is_filtered[None, :, None], smooth_rows, flat_increment)
    return (flat_fields + final_increment).reshape(fields.shape)


def solution(mesh):
    placed = (P(None, None, "lat", "lon"), P(None, "lat", "lon"), P(None, "lat", "lon"), P(), P())
    return jax.shard_map(
        body, mesh=mesh, in_specs=placed, out_specs=P(None, None, "lat", "lon"), check_vma=False
    )
```

```python
from functools import partial
import math

import jax
import jax.numpy as jnp
from jax import lax
from jax.sharding import PartitionSpec as P

radix_len = 128


def phase_table(row_total, col_total, modulus):
    product = (
        jnp.arange(row_total, dtype=jnp.int32)[:, None]
        * jnp.arange(col_total, dtype=jnp.int32)[None, :]
        % modulus
    )
    angle = product.astype(jnp.float32) * (2.0 * math.pi / modulus)
    return (jnp.cos(angle), jnp.sin(angle))


def filter_lines(lines, line_cut):
    line_total, circle = lines.shape
    outer = circle // radix_len
    mixer = partial(jnp.einsum, precision=lax.Precision.HIGHEST)
    outer_cos, outer_sin = phase_table(outer, outer, outer)
    inner_cos, inner_sin = phase_table(radix_len, radix_len, radix_len)
    twist_cos, twist_sin = phase_table(outer, radix_len, circle)
    values = lines.reshape(line_total, outer, radix_len)
    first_re = mixer("lan,aj->ljn", values, outer_cos)
    first_im = -mixer("lan,aj->ljn", values, outer_sin)
    turned_re = first_re * twist_cos + first_im * twist_sin
    turned_im = first_im * twist_cos - first_re * twist_sin
    spec_re = mixer("ljn,nk->ljk", turned_re, inner_cos) + mixer(
        "ljn,nk->ljk", turned_im, inner_sin
    )
    spec_im = mixer("ljn,nk->ljk", turned_im, inner_cos) - mixer(
        "ljn,nk->ljk", turned_re, inner_sin
    )
    wave = (
        jnp.arange(outer, dtype=jnp.int32)[:, None]
        + outer * jnp.arange(radix_len, dtype=jnp.int32)[None, :]
    )
    mode_value = jnp.minimum(wave, circle - wave).astype(jnp.float32)[None]
    cut_value = line_cut[:, None, None]
    damp = jnp.where(mode_value <= cut_value, 1.0, (cut_value / jnp.maximum(mode_value, 1.0)) ** 2)
    spec_re = spec_re * damp
    spec_im = spec_im * damp
    back_re = mixer("ljk,kn->ljn", spec_re, inner_cos) - mixer("ljk,kn->ljn", spec_im, inner_sin)
    back_im = mixer("ljk,kn->ljn", spec_im, inner_cos) + mixer("ljk,kn->ljn", spec_re, inner_sin)
    untwist_re = back_re * twist_cos - back_im * twist_sin
    untwist_im = back_im * twist_cos + back_re * twist_sin
    result = mixer("ljn,ja->lan", untwist_re, outer_cos) - mixer(
        "ljn,ja->lan", untwist_im, outer_sin
    )
    return (result / circle).reshape(line_total, circle)


def face_flux(courant, near_value, far_value):
    return 0.5 * courant * (near_value + far_value) - 0.5 * courant * courant * (
        far_value - near_value
    )


def body(fields, lon_courant, lat_courant, filter_rows, cutoff):
    field_count, level_count, rows_dev, columns = fields.shape
    stacked = field_count * level_count
    lon_devices = lax.axis_size("lon")
    lat_devices = lax.axis_size("lat")
    flat_fields = fields.reshape(stacked, rows_dev, columns)
    eastward = [(i, (i + 1) % lon_devices) for i in range(lon_devices)]
    westward = [((i + 1) % lon_devices, i) for i in range(lon_devices)]
    northward = [(i, i + 1) for i in range(lat_devices - 1)]
    southward = [(i + 1, i) for i in range(lat_devices - 1)]
    from_west = lax.ppermute(
        jnp.concatenate([flat_fields[..., -1], lon_courant[..., -1]], axis=0), "lon", eastward
    )
    from_east = lax.ppermute(flat_fields[..., 0], "lon", westward)
    from_below = lax.ppermute(
        jnp.concatenate([flat_fields[:, -1], lat_courant[:, -1]], axis=0), "lat", northward
    )
    from_above = lax.ppermute(flat_fields[:, 0], "lat", southward)
    wide_fields = jnp.concatenate(
        [from_west[:stacked, :, None], flat_fields, from_east[:, :, None]], axis=2
    ).reshape(field_count, level_count, rows_dev, columns + 2)
    wide_courant = jnp.concatenate([from_west[stacked:, :, None], lon_courant], axis=2)
    column_flux = face_flux(wide_courant, wide_fields[..., :-1], wide_fields[..., 1:])
    tall_fields = jnp.concatenate(
        [from_below[:stacked, None], flat_fields, from_above[:, None]], axis=1
    ).reshape(field_count, level_count, rows_dev + 2, columns)
    tall_courant = jnp.concatenate([from_below[stacked:, None], lat_courant], axis=1)
    row_flux = face_flux(tall_courant, tall_fields[:, :, :-1], tall_fields[:, :, 1:])
    tile_index = lax.axis_index("lat")
    lower_row = tile_index * rows_dev - 1 + jnp.arange(rows_dev + 1, dtype=jnp.int32)
    row_flux = jnp.where((lower_row == rows_dev * lat_devices - 1)[:, None], 0.0, row_flux)
    increment = -(column_flux[..., 1:] - column_flux[..., :-1]) - (
        row_flux[:, :, 1:] - row_flux[:, :, :-1]
    )
    flat_increment = increment.reshape(stacked, rows_dev, columns)
    half_rows = rows_dev // 2
    pair_shift = lat_devices // 2
    pair_perm = [(i, (i + pair_shift) % lat_devices) for i in range(lat_devices)]
    is_low = tile_index < pair_shift
    partner_index = (tile_index + pair_shift) % lat_devices

    def row_info(tile):
        row_global = tile * rows_dev + jnp.arange(rows_dev, dtype=jnp.int32)
        matched = filter_rows[None, :] == row_global[:, None]
        return jnp.any(matched, axis=1), jnp.sum(jnp.where(matched, cutoff[None, :], 0), axis=1)

    is_filtered, own_cut = row_info(tile_index)
    _, partner_cut = row_info(partner_index)
    row_cut = jnp.where(is_filtered, own_cut, partner_cut).astype(jnp.float32)
    low_half = flat_increment[:, :half_rows]
    high_half = flat_increment[:, half_rows:]
    kept = jnp.where(is_low, low_half, high_half)
    given = jnp.where(is_low, high_half, low_half)
    kept_filtered = jnp.where(is_low, is_filtered[:half_rows], is_filtered[half_rows:])
    kept_cut = jnp.where(is_low, row_cut[:half_rows], row_cut[half_rows:])
    chunk_sizes = (stacked * 2 // 5, stacked - stacked * 2 // 5)
    returned_parts, handed_parts = [], []
    chunk_start = 0
    for chunk_stack in chunk_sizes:
        rows_of_part = slice(chunk_start, chunk_start + chunk_stack)
        chunk_start += chunk_stack
        line_count = chunk_stack * half_rows // lon_devices
        line_index = lax.axis_index("lon") * line_count + jnp.arange(line_count, dtype=jnp.int32)
        line_cut = kept_cut[line_index % half_rows]
        taken = lax.ppermute(given[rows_of_part], "lat", pair_perm)
        pair_lines = jnp.where(kept_filtered[None, :, None], kept[rows_of_part], taken)
        full_lines = lax.all_to_all(
            pair_lines.reshape(chunk_stack * half_rows, columns),
            "lon",
            split_axis=0,
            concat_axis=1,
            tiled=True,
        )
        smoothed = filter_lines(full_lines, line_cut)
        returned = lax.all_to_all(
            smoothed, "lon", split_axis=1, concat_axis=0, tiled=True
        ).reshape(chunk_stack, half_rows, columns)
        returned_parts.append(returned)
        handed_parts.append(lax.ppermute(returned, "lat", pair_perm))
    returned = jnp.concatenate(returned_parts, axis=0)
    handed_back = jnp.concatenate(handed_parts, axis=0)
    smooth_rows = jnp.where(
        is_low,
        jnp.concatenate([returned, handed_back], axis=1),
        jnp.concatenate([handed_back, returned], axis=1),
    )
    final_increment = jnp.where(is_filtered[None, :, None], smooth_rows, flat_increment)
    return (flat_fields + final_increment).reshape(fields.shape)


def solution(mesh):
    placed = (P(None, None, "lat", "lon"), P(None, "lat", "lon"), P(None, "lat", "lon"), P(), P())
    return jax.shard_map(
        body, mesh=mesh, in_specs=placed, out_specs=P(None, None, "lat", "lon"), check_vma=False
    )
```

```python
from functools import partial
import math

import jax
import jax.numpy as jnp
from jax import lax
from jax.sharding import PartitionSpec as P

radix_len = 128


def phase_table(row_total, col_total, modulus):
    product = (
        jnp.arange(row_total, dtype=jnp.int32)[:, None]
        * jnp.arange(col_total, dtype=jnp.int32)[None, :]
        % modulus
    )
    angle = product.astype(jnp.float32) * (2.0 * math.pi / modulus)
    return (jnp.cos(angle), jnp.sin(angle))


def filter_lines(lines, line_cut):
    line_total, circle = lines.shape
    outer = circle // radix_len
    mixer = partial(jnp.einsum, precision=lax.Precision.HIGHEST)
    outer_cos, outer_sin = phase_table(outer, outer, outer)
    inner_cos, inner_sin = phase_table(radix_len, radix_len, radix_len)
    twist_cos, twist_sin = phase_table(outer, radix_len, circle)
    values = lines.reshape(line_total, outer, radix_len)
    first_re = mixer("lan,aj->ljn", values, outer_cos)
    first_im = -mixer("lan,aj->ljn", values, outer_sin)
    turned_re = first_re * twist_cos + first_im * twist_sin
    turned_im = first_im * twist_cos - first_re * twist_sin
    spec_re = mixer("ljn,nk->ljk", turned_re, inner_cos) + mixer(
        "ljn,nk->ljk", turned_im, inner_sin
    )
    spec_im = mixer("ljn,nk->ljk", turned_im, inner_cos) - mixer(
        "ljn,nk->ljk", turned_re, inner_sin
    )
    wave = (
        jnp.arange(outer, dtype=jnp.int32)[:, None]
        + outer * jnp.arange(radix_len, dtype=jnp.int32)[None, :]
    )
    mode_value = jnp.minimum(wave, circle - wave).astype(jnp.float32)[None]
    cut_value = line_cut[:, None, None]
    damp = jnp.where(mode_value <= cut_value, 1.0, (cut_value / jnp.maximum(mode_value, 1.0)) ** 2)
    spec_re = spec_re * damp
    spec_im = spec_im * damp
    back_re = mixer("ljk,kn->ljn", spec_re, inner_cos) - mixer("ljk,kn->ljn", spec_im, inner_sin)
    back_im = mixer("ljk,kn->ljn", spec_im, inner_cos) + mixer("ljk,kn->ljn", spec_re, inner_sin)
    untwist_re = back_re * twist_cos - back_im * twist_sin
    untwist_im = back_im * twist_cos + back_re * twist_sin
    result = mixer("ljn,ja->lan", untwist_re, outer_cos) - mixer(
        "ljn,ja->lan", untwist_im, outer_sin
    )
    return (result / circle).reshape(line_total, circle)


def face_flux(courant, near_value, far_value):
    return 0.5 * courant * (near_value + far_value) - 0.5 * courant * courant * (
        far_value - near_value
    )


def body(fields, lon_courant, lat_courant, filter_rows, cutoff):
    field_count, level_count, rows_dev, columns = fields.shape
    stacked = field_count * level_count
    lon_devices = lax.axis_size("lon")
    lat_devices = lax.axis_size("lat")
    flat_fields = fields.reshape(stacked, rows_dev, columns)
    eastward = [(i, (i + 1) % lon_devices) for i in range(lon_devices)]
    westward = [((i + 1) % lon_devices, i) for i in range(lon_devices)]
    northward = [(i, i + 1) for i in range(lat_devices - 1)]
    southward = [(i + 1, i) for i in range(lat_devices - 1)]
    from_west = lax.ppermute(
        jnp.concatenate([flat_fields[..., -1], lon_courant[..., -1]], axis=0), "lon", eastward
    )
    from_east = lax.ppermute(flat_fields[..., 0], "lon", westward)
    from_below = lax.ppermute(
        jnp.concatenate([flat_fields[:, -1], lat_courant[:, -1]], axis=0), "lat", northward
    )
    from_above = lax.ppermute(flat_fields[:, 0], "lat", southward)
    tile_index = lax.axis_index("lat")
    column = jnp.arange(columns, dtype=jnp.int32)
    row = jnp.arange(rows_dev, dtype=jnp.int32)[:, None]
    west_fields = from_west[:stacked].reshape(field_count, level_count, rows_dev)
    east_fields = from_east.reshape(field_count, level_count, rows_dev)
    right = jnp.where(column == columns - 1, east_fields[..., None], jnp.roll(fields, -1, axis=3))
    east_flux = face_flux(lon_courant, fields, right)
    west_edge = face_flux(from_west[stacked:], west_fields, fields[..., 0])
    west_flux = jnp.where(column == 0, west_edge[..., None], jnp.roll(east_flux, 1, axis=3))
    below_fields = from_below[:stacked].reshape(field_count, level_count, columns)
    above_fields = from_above.reshape(field_count, level_count, columns)
    upper = jnp.where(row == rows_dev - 1, above_fields[:, :, None], jnp.roll(fields, -1, axis=2))
    north_flux = face_flux(lat_courant, fields, upper)
    top_face = (tile_index == lat_devices - 1) & (row == rows_dev - 1)
    north_flux = jnp.where(top_face, 0.0, north_flux)
    south_edge = face_flux(from_below[stacked:], below_fields, fields[:, :, 0])
    south_flux = jnp.where(row == 0, south_edge[:, :, None], jnp.roll(north_flux, 1, axis=2))
    increment = -(east_flux - west_flux) - (north_flux - south_flux)
    flat_increment = increment.reshape(stacked, rows_dev, columns)
    half_rows = rows_dev // 2
    pair_shift = lat_devices // 2
    pair_perm = [(i, (i + pair_shift) % lat_devices) for i in range(lat_devices)]
    is_low = tile_index < pair_shift
    partner_index = (tile_index + pair_shift) % lat_devices

    def row_info(tile):
        row_global = tile * rows_dev + jnp.arange(rows_dev, dtype=jnp.int32)
        matched = filter_rows[None, :] == row_global[:, None]
        return jnp.any(matched, axis=1), jnp.sum(jnp.where(matched, cutoff[None, :], 0), axis=1)

    is_filtered, own_cut = row_info(tile_index)
    _, partner_cut = row_info(partner_index)
    row_cut = jnp.where(is_filtered, own_cut, partner_cut).astype(jnp.float32)
    low_half = flat_increment[:, :half_rows]
    high_half = flat_increment[:, half_rows:]
    kept = jnp.where(is_low, low_half, high_half)
    given = jnp.where(is_low, high_half, low_half)
    kept_filtered = jnp.where(is_low, is_filtered[:half_rows], is_filtered[half_rows:])
    kept_cut = jnp.where(is_low, row_cut[:half_rows], row_cut[half_rows:])
    chunk_sizes = (stacked * 2 // 5, stacked - stacked * 2 // 5)
    returned_parts, handed_parts = [], []
    chunk_start = 0
    for chunk_stack in chunk_sizes:
        rows_of_part = slice(chunk_start, chunk_start + chunk_stack)
        chunk_start += chunk_stack
        line_count = chunk_stack * half_rows // lon_devices
        line_index = lax.axis_index("lon") * line_count + jnp.arange(line_count, dtype=jnp.int32)
        line_cut = kept_cut[line_index % half_rows]
        taken = lax.ppermute(given[rows_of_part], "lat", pair_perm)
        pair_lines = jnp.where(kept_filtered[None, :, None], kept[rows_of_part], taken)
        full_lines = lax.all_to_all(
            pair_lines.reshape(chunk_stack * half_rows, columns),
            "lon",
            split_axis=0,
            concat_axis=1,
            tiled=True,
        )
        smoothed = filter_lines(full_lines, line_cut)
        returned = lax.all_to_all(
            smoothed, "lon", split_axis=1, concat_axis=0, tiled=True
        ).reshape(chunk_stack, half_rows, columns)
        returned_parts.append(returned)
        handed_parts.append(lax.ppermute(returned, "lat", pair_perm))
    returned = jnp.concatenate(returned_parts, axis=0)
    handed_back = jnp.concatenate(handed_parts, axis=0)
    smooth_rows = jnp.where(
        is_low,
        jnp.concatenate([returned, handed_back], axis=1),
        jnp.concatenate([handed_back, returned], axis=1),
    )
    final_increment = jnp.where(is_filtered[None, :, None], smooth_rows, flat_increment)
    return (flat_fields + final_increment).reshape(fields.shape)


def solution(mesh):
    placed = (P(None, None, "lat", "lon"), P(None, "lat", "lon"), P(None, "lat", "lon"), P(), P())
    return jax.shard_map(
        body, mesh=mesh, in_specs=placed, out_specs=P(None, None, "lat", "lon"), check_vma=False
    )
```

```python
from functools import partial
import math

import jax
import jax.numpy as jnp
from jax import lax
from jax.sharding import PartitionSpec as P

radix_len = 128


def phase_table(row_total, col_total, modulus):
    product = (
        jnp.arange(row_total, dtype=jnp.int32)[:, None]
        * jnp.arange(col_total, dtype=jnp.int32)[None, :]
        % modulus
    )
    angle = product.astype(jnp.float32) * (2.0 * math.pi / modulus)
    return (jnp.cos(angle), jnp.sin(angle))


def filter_lines(lines, line_cut):
    line_total, circle = lines.shape
    outer = circle // radix_len
    mixer = partial(jnp.einsum, precision=lax.Precision.HIGH)
    outer_cos, outer_sin = phase_table(outer, outer, outer)
    inner_cos, inner_sin = phase_table(radix_len, radix_len, radix_len)
    twist_cos, twist_sin = phase_table(outer, radix_len, circle)
    values = lines.reshape(line_total, outer, radix_len)
    first_re = mixer("lan,aj->ljn", values, outer_cos)
    first_im = -mixer("lan,aj->ljn", values, outer_sin)
    turned_re = first_re * twist_cos + first_im * twist_sin
    turned_im = first_im * twist_cos - first_re * twist_sin
    spec_re = mixer("ljn,nk->ljk", turned_re, inner_cos) + mixer(
        "ljn,nk->ljk", turned_im, inner_sin
    )
    spec_im = mixer("ljn,nk->ljk", turned_im, inner_cos) - mixer(
        "ljn,nk->ljk", turned_re, inner_sin
    )
    wave = (
        jnp.arange(outer, dtype=jnp.int32)[:, None]
        + outer * jnp.arange(radix_len, dtype=jnp.int32)[None, :]
    )
    mode_value = jnp.minimum(wave, circle - wave).astype(jnp.float32)[None]
    cut_value = line_cut[:, None, None]
    damp = jnp.where(mode_value <= cut_value, 1.0, (cut_value / jnp.maximum(mode_value, 1.0)) ** 2)
    spec_re = spec_re * damp
    spec_im = spec_im * damp
    back_re = mixer("ljk,kn->ljn", spec_re, inner_cos) - mixer("ljk,kn->ljn", spec_im, inner_sin)
    back_im = mixer("ljk,kn->ljn", spec_im, inner_cos) + mixer("ljk,kn->ljn", spec_re, inner_sin)
    untwist_re = back_re * twist_cos - back_im * twist_sin
    untwist_im = back_im * twist_cos + back_re * twist_sin
    result = mixer("ljn,ja->lan", untwist_re, outer_cos) - mixer(
        "ljn,ja->lan", untwist_im, outer_sin
    )
    return (result / circle).reshape(line_total, circle)


def face_flux(courant, near_value, far_value):
    return 0.5 * courant * (near_value + far_value) - 0.5 * courant * courant * (
        far_value - near_value
    )


def body(fields, lon_courant, lat_courant, filter_rows, cutoff):
    field_count, level_count, rows_dev, columns = fields.shape
    stacked = field_count * level_count
    lon_devices = lax.axis_size("lon")
    lat_devices = lax.axis_size("lat")
    flat_fields = fields.reshape(stacked, rows_dev, columns)
    eastward = [(i, (i + 1) % lon_devices) for i in range(lon_devices)]
    westward = [((i + 1) % lon_devices, i) for i in range(lon_devices)]
    northward = [(i, i + 1) for i in range(lat_devices - 1)]
    southward = [(i + 1, i) for i in range(lat_devices - 1)]
    from_west = lax.ppermute(
        jnp.concatenate([flat_fields[..., -1], lon_courant[..., -1]], axis=0), "lon", eastward
    )
    from_east = lax.ppermute(flat_fields[..., 0], "lon", westward)
    from_below = lax.ppermute(
        jnp.concatenate([flat_fields[:, -1], lat_courant[:, -1]], axis=0), "lat", northward
    )
    from_above = lax.ppermute(flat_fields[:, 0], "lat", southward)
    wide_fields = jnp.concatenate(
        [from_west[:stacked, :, None], flat_fields, from_east[:, :, None]], axis=2
    ).reshape(field_count, level_count, rows_dev, columns + 2)
    wide_courant = jnp.concatenate([from_west[stacked:, :, None], lon_courant], axis=2)
    column_flux = face_flux(wide_courant, wide_fields[..., :-1], wide_fields[..., 1:])
    tall_fields = jnp.concatenate(
        [from_below[:stacked, None], flat_fields, from_above[:, None]], axis=1
    ).reshape(field_count, level_count, rows_dev + 2, columns)
    tall_courant = jnp.concatenate([from_below[stacked:, None], lat_courant], axis=1)
    row_flux = face_flux(tall_courant, tall_fields[:, :, :-1], tall_fields[:, :, 1:])
    tile_index = lax.axis_index("lat")
    lower_row = tile_index * rows_dev - 1 + jnp.arange(rows_dev + 1, dtype=jnp.int32)
    row_flux = jnp.where((lower_row == rows_dev * lat_devices - 1)[:, None], 0.0, row_flux)
    increment = -(column_flux[..., 1:] - column_flux[..., :-1]) - (
        row_flux[:, :, 1:] - row_flux[:, :, :-1]
    )
    flat_increment = increment.reshape(stacked, rows_dev, columns)
    half_rows = rows_dev // 2
    pair_shift = lat_devices // 2
    pair_perm = [(i, (i + pair_shift) % lat_devices) for i in range(lat_devices)]
    is_low = tile_index < pair_shift
    partner_index = (tile_index + pair_shift) % lat_devices

    def row_info(tile):
        row_global = tile * rows_dev + jnp.arange(rows_dev, dtype=jnp.int32)
        matched = filter_rows[None, :] == row_global[:, None]
        return jnp.any(matched, axis=1), jnp.sum(jnp.where(matched, cutoff[None, :], 0), axis=1)

    is_filtered, own_cut = row_info(tile_index)
    _, partner_cut = row_info(partner_index)
    row_cut = jnp.where(is_filtered, own_cut, partner_cut).astype(jnp.float32)
    low_half = flat_increment[:, :half_rows]
    high_half = flat_increment[:, half_rows:]
    kept = jnp.where(is_low, low_half, high_half)
    given = jnp.where(is_low, high_half, low_half)
    kept_filtered = jnp.where(is_low, is_filtered[:half_rows], is_filtered[half_rows:])
    kept_cut = jnp.where(is_low, row_cut[:half_rows], row_cut[half_rows:])
    chunk_sizes = (stacked * 2 // 5, stacked - stacked * 2 // 5)
    returned_parts, handed_parts = [], []
    chunk_start = 0
    for chunk_stack in chunk_sizes:
        rows_of_part = slice(chunk_start, chunk_start + chunk_stack)
        chunk_start += chunk_stack
        line_count = chunk_stack * half_rows // lon_devices
        line_index = lax.axis_index("lon") * line_count + jnp.arange(line_count, dtype=jnp.int32)
        line_cut = kept_cut[line_index % half_rows]
        taken = lax.ppermute(given[rows_of_part], "lat", pair_perm)
        pair_lines = jnp.where(kept_filtered[None, :, None], kept[rows_of_part], taken)
        full_lines = lax.all_to_all(
            pair_lines.reshape(chunk_stack * half_rows, columns),
            "lon",
            split_axis=0,
            concat_axis=1,
            tiled=True,
        )
        smoothed = filter_lines(full_lines, line_cut)
        returned = lax.all_to_all(
            smoothed, "lon", split_axis=1, concat_axis=0, tiled=True
        ).reshape(chunk_stack, half_rows, columns)
        returned_parts.append(returned)
        handed_parts.append(lax.ppermute(returned, "lat", pair_perm))
    returned = jnp.concatenate(returned_parts, axis=0)
    handed_back = jnp.concatenate(handed_parts, axis=0)
    smooth_rows = jnp.where(
        is_low,
        jnp.concatenate([returned, handed_back], axis=1),
        jnp.concatenate([handed_back, returned], axis=1),
    )
    final_increment = jnp.where(is_filtered[None, :, None], smooth_rows, flat_increment)
    return (flat_fields + final_increment).reshape(fields.shape)


def solution(mesh):
    placed = (P(None, None, "lat", "lon"), P(None, "lat", "lon"), P(None, "lat", "lon"), P(), P())
    return jax.shard_map(
        body, mesh=mesh, in_specs=placed, out_specs=P(None, None, "lat", "lon"), check_vma=False
    )
```

```python
from functools import partial
import math

import jax
import jax.numpy as jnp
from jax import lax
from jax.sharding import PartitionSpec as P

radix_len = 128


def phase_table(row_total, col_total, modulus):
    product = (
        jnp.arange(row_total, dtype=jnp.int32)[:, None]
        * jnp.arange(col_total, dtype=jnp.int32)[None, :]
        % modulus
    )
    angle = product.astype(jnp.float32) * (2.0 * math.pi / modulus)
    return (jnp.cos(angle), jnp.sin(angle))


def filter_lines(lines, line_cut):
    line_total, circle = lines.shape
    outer = circle // radix_len
    mixer = partial(jnp.einsum, precision=lax.Precision.HIGH)
    outer_cos, outer_sin = phase_table(outer, outer, outer)
    inner_cos, inner_sin = phase_table(radix_len, radix_len, radix_len)
    twist_cos, twist_sin = phase_table(outer, radix_len, circle)
    values = lines.reshape(line_total, outer, radix_len)
    first_re = mixer("lan,aj->ljn", values, outer_cos)
    first_im = -mixer("lan,aj->ljn", values, outer_sin)
    turned_re = first_re * twist_cos + first_im * twist_sin
    turned_im = first_im * twist_cos - first_re * twist_sin
    spec_re = mixer("ljn,nk->ljk", turned_re, inner_cos) + mixer(
        "ljn,nk->ljk", turned_im, inner_sin
    )
    spec_im = mixer("ljn,nk->ljk", turned_im, inner_cos) - mixer(
        "ljn,nk->ljk", turned_re, inner_sin
    )
    wave = (
        jnp.arange(outer, dtype=jnp.int32)[:, None]
        + outer * jnp.arange(radix_len, dtype=jnp.int32)[None, :]
    )
    mode_value = jnp.minimum(wave, circle - wave).astype(jnp.float32)[None]
    cut_value = line_cut[:, None, None]
    damp = jnp.where(mode_value <= cut_value, 1.0, (cut_value / jnp.maximum(mode_value, 1.0)) ** 2)
    spec_re = spec_re * damp
    spec_im = spec_im * damp
    back_re = mixer("ljk,kn->ljn", spec_re, inner_cos) - mixer("ljk,kn->ljn", spec_im, inner_sin)
    back_im = mixer("ljk,kn->ljn", spec_im, inner_cos) + mixer("ljk,kn->ljn", spec_re, inner_sin)
    untwist_re = back_re * twist_cos - back_im * twist_sin
    untwist_im = back_im * twist_cos + back_re * twist_sin
    result = mixer("ljn,ja->lan", untwist_re, outer_cos) - mixer(
        "ljn,ja->lan", untwist_im, outer_sin
    )
    return (result / circle).reshape(line_total, circle)


def face_flux(courant, near_value, far_value):
    return 0.5 * courant * (near_value + far_value) - 0.5 * courant * courant * (
        far_value - near_value
    )


def body(fields, lon_courant, lat_courant, filter_rows, cutoff):
    field_count, level_count, rows_dev, columns = fields.shape
    stacked = field_count * level_count
    lon_devices = lax.axis_size("lon")
    lat_devices = lax.axis_size("lat")
    flat_fields = fields.reshape(stacked, rows_dev, columns)
    eastward = [(i, (i + 1) % lon_devices) for i in range(lon_devices)]
    westward = [((i + 1) % lon_devices, i) for i in range(lon_devices)]
    northward = [(i, i + 1) for i in range(lat_devices - 1)]
    southward = [(i + 1, i) for i in range(lat_devices - 1)]
    from_west = lax.ppermute(
        jnp.concatenate([flat_fields[..., -1], lon_courant[..., -1]], axis=0), "lon", eastward
    )
    from_east = lax.ppermute(flat_fields[..., 0], "lon", westward)
    from_below = lax.ppermute(
        jnp.concatenate([flat_fields[:, -1], lat_courant[:, -1]], axis=0), "lat", northward
    )
    from_above = lax.ppermute(flat_fields[:, 0], "lat", southward)
    tile_index = lax.axis_index("lat")
    column = jnp.arange(columns, dtype=jnp.int32)
    row = jnp.arange(rows_dev, dtype=jnp.int32)[:, None]
    local_right = jnp.concatenate([fields[..., 1:], jnp.zeros_like(fields[..., :1])], axis=3)
    local_east = face_flux(lon_courant, fields, local_right)
    local_west = jnp.concatenate([jnp.zeros_like(local_east[..., :1]), local_east[..., :-1]], axis=3)
    local_upper = jnp.concatenate([fields[:, :, 1:], jnp.zeros_like(fields[:, :, :1])], axis=2)
    top_face = (tile_index == lat_devices - 1) & (row == rows_dev - 1)
    local_north = jnp.where(top_face, 0.0, face_flux(lat_courant, fields, local_upper))
    local_south = jnp.concatenate(
        [jnp.zeros_like(local_north[:, :, :1]), local_north[:, :, :-1]], axis=2
    )
    local_increment = -(local_east - local_west) - (local_north - local_south)
    west_fields = from_west[:stacked].reshape(field_count, level_count, rows_dev)
    east_fields = from_east.reshape(field_count, level_count, rows_dev)
    west_edge = face_flux(from_west[stacked:], west_fields, fields[..., 0])
    east_change = face_flux(
        lon_courant[..., -1], fields[..., -1], east_fields
    ) - face_flux(lon_courant[..., -1], fields[..., -1], 0.0)
    below_fields = from_below[:stacked].reshape(field_count, level_count, columns)
    above_fields = from_above.reshape(field_count, level_count, columns)
    south_edge = face_flux(from_below[stacked:], below_fields, fields[:, :, 0])
    top_tile = tile_index == lat_devices - 1
    north_change = jnp.where(
        top_tile,
        0.0,
        face_flux(lat_courant[:, -1], fields[:, :, -1], above_fields)
        - face_flux(lat_courant[:, -1], fields[:, :, -1], 0.0),
    )
    edge_change = (
        jnp.where(column == 0, west_edge[..., None], 0.0)
        - jnp.where(column == columns - 1, east_change[..., None], 0.0)
        + jnp.where(row == 0, south_edge[:, :, None], 0.0)
        - jnp.where(row == rows_dev - 1, north_change[:, :, None], 0.0)
    )
    increment = local_increment + edge_change
    flat_increment = increment.reshape(stacked, rows_dev, columns)
    half_rows = rows_dev // 2
    pair_shift = lat_devices // 2
    pair_perm = [(i, (i + pair_shift) % lat_devices) for i in range(lat_devices)]
    is_low = tile_index < pair_shift
    partner_index = (tile_index + pair_shift) % lat_devices

    def row_info(tile):
        row_global = tile * rows_dev + jnp.arange(rows_dev, dtype=jnp.int32)
        matched = filter_rows[None, :] == row_global[:, None]
        return jnp.any(matched, axis=1), jnp.sum(jnp.where(matched, cutoff[None, :], 0), axis=1)

    is_filtered, own_cut = row_info(tile_index)
    _, partner_cut = row_info(partner_index)
    row_cut = jnp.where(is_filtered, own_cut, partner_cut).astype(jnp.float32)
    low_half = flat_increment[:, :half_rows]
    high_half = flat_increment[:, half_rows:]
    kept = jnp.where(is_low, low_half, high_half)
    given = jnp.where(is_low, high_half, low_half)
    kept_filtered = jnp.where(is_low, is_filtered[:half_rows], is_filtered[half_rows:])
    kept_cut = jnp.where(is_low, row_cut[:half_rows], row_cut[half_rows:])
    chunk_sizes = (stacked * 2 // 5, stacked - stacked * 2 // 5)
    returned_parts, handed_parts = [], []
    chunk_start = 0
    for chunk_stack in chunk_sizes:
        rows_of_part = slice(chunk_start, chunk_start + chunk_stack)
        chunk_start += chunk_stack
        line_count = chunk_stack * half_rows // lon_devices
        line_index = lax.axis_index("lon") * line_count + jnp.arange(line_count, dtype=jnp.int32)
        line_cut = kept_cut[line_index % half_rows]
        taken = lax.ppermute(given[rows_of_part], "lat", pair_perm)
        pair_lines = jnp.where(kept_filtered[None, :, None], kept[rows_of_part], taken)
        full_lines = lax.all_to_all(
            pair_lines.reshape(chunk_stack * half_rows, columns),
            "lon",
            split_axis=0,
            concat_axis=1,
            tiled=True,
        )
        smoothed = filter_lines(full_lines, line_cut)
        returned = lax.all_to_all(
            smoothed, "lon", split_axis=1, concat_axis=0, tiled=True
        ).reshape(chunk_stack, half_rows, columns)
        returned_parts.append(returned)
        handed_parts.append(lax.ppermute(returned, "lat", pair_perm))
    returned = jnp.concatenate(returned_parts, axis=0)
    handed_back = jnp.concatenate(handed_parts, axis=0)
    smooth_rows = jnp.where(
        is_low,
        jnp.concatenate([returned, handed_back], axis=1),
        jnp.concatenate([handed_back, returned], axis=1),
    )
    final_increment = jnp.where(is_filtered[None, :, None], smooth_rows, flat_increment)
    return (flat_fields + final_increment).reshape(fields.shape)


def solution(mesh):
    placed = (P(None, None, "lat", "lon"), P(None, "lat", "lon"), P(None, "lat", "lon"), P(), P())
    return jax.shard_map(
        body, mesh=mesh, in_specs=placed, out_specs=P(None, None, "lat", "lon"), check_vma=False
    )
```

```python
from functools import partial
import math

import jax
import jax.numpy as jnp
from jax import lax
from jax.sharding import PartitionSpec as P

radix_len = 128


def phase_table(row_total, col_total, modulus):
    product = (
        jnp.arange(row_total, dtype=jnp.int32)[:, None]
        * jnp.arange(col_total, dtype=jnp.int32)[None, :]
        % modulus
    )
    angle = product.astype(jnp.float32) * (2.0 * math.pi / modulus)
    return (jnp.cos(angle), jnp.sin(angle))


def filter_lines(lines, line_cut):
    line_total, circle = lines.shape
    outer = circle // radix_len
    mixer = partial(jnp.einsum, precision=lax.Precision.HIGH)
    outer_cos, outer_sin = phase_table(outer, outer, outer)
    inner_cos, inner_sin = phase_table(radix_len, radix_len, radix_len)
    twist_cos, twist_sin = phase_table(outer, radix_len, circle)
    forward_outer = jnp.concatenate([outer_cos, -outer_sin], axis=1)
    forward_inner = jnp.concatenate(
        [
            jnp.concatenate([inner_cos, -inner_sin], axis=1),
            jnp.concatenate([inner_sin, inner_cos], axis=1),
        ],
        axis=0,
    )
    inverse_inner = jnp.concatenate(
        [
            jnp.concatenate([inner_cos, inner_sin], axis=1),
            jnp.concatenate([-inner_sin, inner_cos], axis=1),
        ],
        axis=0,
    )
    inverse_outer = jnp.concatenate([outer_cos, -outer_sin], axis=0)
    values = lines.reshape(line_total, outer, radix_len)
    first = mixer("lan,ab->lbn", values, forward_outer)
    first_re, first_im = first[:, :outer], first[:, outer:]
    turned = jnp.concatenate(
        [first_re * twist_cos + first_im * twist_sin, first_im * twist_cos - first_re * twist_sin],
        axis=2,
    )
    spectrum = mixer("ljn,nk->ljk", turned, forward_inner)
    wave = (
        jnp.arange(outer, dtype=jnp.int32)[:, None]
        + outer * jnp.arange(radix_len, dtype=jnp.int32)[None, :]
    )
    mode_value = jnp.minimum(wave, circle - wave).astype(jnp.float32)[None]
    cut_value = line_cut[:, None, None]
    damp = jnp.where(mode_value <= cut_value, 1.0, (cut_value / jnp.maximum(mode_value, 1.0)) ** 2)
    spectrum = spectrum * jnp.concatenate([damp, damp], axis=2)
    back = mixer("ljk,kn->ljn", spectrum, inverse_inner)
    back_re, back_im = back[..., :radix_len], back[..., radix_len:]
    untwisted = jnp.concatenate(
        [back_re * twist_cos - back_im * twist_sin, back_im * twist_cos + back_re * twist_sin],
        axis=1,
    )
    result = mixer("lbn,ba->lan", untwisted, inverse_outer)
    return (result / circle).reshape(line_total, circle)


def face_flux(courant, near_value, far_value):
    return 0.5 * courant * (near_value + far_value) - 0.5 * courant * courant * (
        far_value - near_value
    )


def body(fields, lon_courant, lat_courant, filter_rows, cutoff):
    field_count, level_count, rows_dev, columns = fields.shape
    stacked = field_count * level_count
    lon_devices = lax.axis_size("lon")
    lat_devices = lax.axis_size("lat")
    flat_fields = fields.reshape(stacked, rows_dev, columns)
    eastward = [(i, (i + 1) % lon_devices) for i in range(lon_devices)]
    westward = [((i + 1) % lon_devices, i) for i in range(lon_devices)]
    northward = [(i, i + 1) for i in range(lat_devices - 1)]
    southward = [(i + 1, i) for i in range(lat_devices - 1)]
    from_west = lax.ppermute(
        jnp.concatenate([flat_fields[..., -1], lon_courant[..., -1]], axis=0), "lon", eastward
    )
    from_east = lax.ppermute(flat_fields[..., 0], "lon", westward)
    from_below = lax.ppermute(
        jnp.concatenate([flat_fields[:, -1], lat_courant[:, -1]], axis=0), "lat", northward
    )
    from_above = lax.ppermute(flat_fields[:, 0], "lat", southward)
    wide_fields = jnp.concatenate(
        [from_west[:stacked, :, None], flat_fields, from_east[:, :, None]], axis=2
    ).reshape(field_count, level_count, rows_dev, columns + 2)
    wide_courant = jnp.concatenate([from_west[stacked:, :, None], lon_courant], axis=2)
    column_flux = face_flux(wide_courant, wide_fields[..., :-1], wide_fields[..., 1:])
    tall_fields = jnp.concatenate(
        [from_below[:stacked, None], flat_fields, from_above[:, None]], axis=1
    ).reshape(field_count, level_count, rows_dev + 2, columns)
    tall_courant = jnp.concatenate([from_below[stacked:, None], lat_courant], axis=1)
    row_flux = face_flux(tall_courant, tall_fields[:, :, :-1], tall_fields[:, :, 1:])
    tile_index = lax.axis_index("lat")
    lower_row = tile_index * rows_dev - 1 + jnp.arange(rows_dev + 1, dtype=jnp.int32)
    row_flux = jnp.where((lower_row == rows_dev * lat_devices - 1)[:, None], 0.0, row_flux)
    increment = -(column_flux[..., 1:] - column_flux[..., :-1]) - (
        row_flux[:, :, 1:] - row_flux[:, :, :-1]
    )
    flat_increment = increment.reshape(stacked, rows_dev, columns)
    half_rows = rows_dev // 2
    pair_shift = lat_devices // 2
    pair_perm = [(i, (i + pair_shift) % lat_devices) for i in range(lat_devices)]
    is_low = tile_index < pair_shift
    partner_index = (tile_index + pair_shift) % lat_devices

    def row_info(tile):
        row_global = tile * rows_dev + jnp.arange(rows_dev, dtype=jnp.int32)
        matched = filter_rows[None, :] == row_global[:, None]
        return jnp.any(matched, axis=1), jnp.sum(jnp.where(matched, cutoff[None, :], 0), axis=1)

    is_filtered, own_cut = row_info(tile_index)
    _, partner_cut = row_info(partner_index)
    row_cut = jnp.where(is_filtered, own_cut, partner_cut).astype(jnp.float32)
    low_half = flat_increment[:, :half_rows]
    high_half = flat_increment[:, half_rows:]
    kept = jnp.where(is_low, low_half, high_half)
    given = jnp.where(is_low, high_half, low_half)
    kept_filtered = jnp.where(is_low, is_filtered[:half_rows], is_filtered[half_rows:])
    kept_cut = jnp.where(is_low, row_cut[:half_rows], row_cut[half_rows:])
    chunk_sizes = (stacked * 2 // 5, stacked - stacked * 2 // 5)
    returned_parts, handed_parts = [], []
    chunk_start = 0
    for chunk_stack in chunk_sizes:
        rows_of_part = slice(chunk_start, chunk_start + chunk_stack)
        chunk_start += chunk_stack
        line_count = chunk_stack * half_rows // lon_devices
        line_index = lax.axis_index("lon") * line_count + jnp.arange(line_count, dtype=jnp.int32)
        line_cut = kept_cut[line_index % half_rows]
        taken = lax.ppermute(given[rows_of_part], "lat", pair_perm)
        pair_lines = jnp.where(kept_filtered[None, :, None], kept[rows_of_part], taken)
        full_lines = lax.all_to_all(
            pair_lines.reshape(chunk_stack * half_rows, columns),
            "lon",
            split_axis=0,
            concat_axis=1,
            tiled=True,
        )
        smoothed = filter_lines(full_lines, line_cut)
        returned = lax.all_to_all(
            smoothed, "lon", split_axis=1, concat_axis=0, tiled=True
        ).reshape(chunk_stack, half_rows, columns)
        returned_parts.append(returned)
        handed_parts.append(lax.ppermute(returned, "lat", pair_perm))
    returned = jnp.concatenate(returned_parts, axis=0)
    handed_back = jnp.concatenate(handed_parts, axis=0)
    smooth_rows = jnp.where(
        is_low,
        jnp.concatenate([returned, handed_back], axis=1),
        jnp.concatenate([handed_back, returned], axis=1),
    )
    final_increment = jnp.where(is_filtered[None, :, None], smooth_rows, flat_increment)
    return (flat_fields + final_increment).reshape(fields.shape)


def solution(mesh):
    placed = (P(None, None, "lat", "lon"), P(None, "lat", "lon"), P(None, "lat", "lon"), P(), P())
    return jax.shard_map(
        body, mesh=mesh, in_specs=placed, out_specs=P(None, None, "lat", "lon"), check_vma=False
    )
```

```python
from functools import partial
import math

import jax
import jax.numpy as jnp
from jax import lax
from jax.sharding import PartitionSpec as P

radix_len = 128


def phase_table(row_total, col_total, modulus):
    product = (
        jnp.arange(row_total, dtype=jnp.int32)[:, None]
        * jnp.arange(col_total, dtype=jnp.int32)[None, :]
        % modulus
    )
    angle = product.astype(jnp.float32) * (2.0 * math.pi / modulus)
    return (jnp.cos(angle), jnp.sin(angle))


def filter_lines(lines, line_cut):
    line_total, circle = lines.shape
    outer = circle // radix_len
    mixer = partial(jnp.einsum, precision=lax.Precision.HIGH)
    outer_cos, outer_sin = phase_table(outer, outer, outer)
    inner_cos, inner_sin = phase_table(radix_len, radix_len, radix_len)
    twist_cos, twist_sin = phase_table(outer, radix_len, circle)
    values = lines.reshape(line_total, outer, radix_len)
    first_re = mixer("lan,aj->ljn", values, outer_cos)
    first_im = -mixer("lan,aj->ljn", values, outer_sin)
    turned_re = first_re * twist_cos + first_im * twist_sin
    turned_im = first_im * twist_cos - first_re * twist_sin
    spec_re = mixer("ljn,nk->ljk", turned_re, inner_cos) + mixer(
        "ljn,nk->ljk", turned_im, inner_sin
    )
    spec_im = mixer("ljn,nk->ljk", turned_im, inner_cos) - mixer(
        "ljn,nk->ljk", turned_re, inner_sin
    )
    wave = (
        jnp.arange(outer, dtype=jnp.int32)[:, None]
        + outer * jnp.arange(radix_len, dtype=jnp.int32)[None, :]
    )
    mode_value = jnp.minimum(wave, circle - wave).astype(jnp.float32)[None]
    cut_value = line_cut[:, None, None]
    damp = jnp.where(mode_value <= cut_value, 1.0, (cut_value / jnp.maximum(mode_value, 1.0)) ** 2)
    spec_re = spec_re * damp
    spec_im = spec_im * damp
    back_re = mixer("ljk,kn->ljn", spec_re, inner_cos) - mixer("ljk,kn->ljn", spec_im, inner_sin)
    back_im = mixer("ljk,kn->ljn", spec_im, inner_cos) + mixer("ljk,kn->ljn", spec_re, inner_sin)
    untwist_re = back_re * twist_cos - back_im * twist_sin
    untwist_im = back_im * twist_cos + back_re * twist_sin
    result = mixer("ljn,ja->lan", untwist_re, outer_cos) - mixer(
        "ljn,ja->lan", untwist_im, outer_sin
    )
    return (result / circle).reshape(line_total, circle)


def face_flux(courant, near_value, far_value):
    return 0.5 * courant * (near_value + far_value) - 0.5 * courant * courant * (
        far_value - near_value
    )


def body(fields, lon_courant, lat_courant, filter_rows, cutoff):
    field_count, level_count, rows_dev, columns = fields.shape
    stacked = field_count * level_count
    lon_devices = lax.axis_size("lon")
    lat_devices = lax.axis_size("lat")
    flat_fields = fields.reshape(stacked, rows_dev, columns)
    eastward = [(i, (i + 1) % lon_devices) for i in range(lon_devices)]
    westward = [((i + 1) % lon_devices, i) for i in range(lon_devices)]
    northward = [(i, i + 1) for i in range(lat_devices - 1)]
    southward = [(i + 1, i) for i in range(lat_devices - 1)]
    from_west = lax.ppermute(
        jnp.concatenate([flat_fields[..., -1], lon_courant[..., -1]], axis=0), "lon", eastward
    )
    from_east = lax.ppermute(flat_fields[..., 0], "lon", westward)
    from_below = lax.ppermute(
        jnp.concatenate([flat_fields[:, -1], lat_courant[:, -1]], axis=0), "lat", northward
    )
    from_above = lax.ppermute(flat_fields[:, 0], "lat", southward)
    tile_index = lax.axis_index("lat")
    lower_row = tile_index * rows_dev - 1 + jnp.arange(rows_dev + 1, dtype=jnp.int32)
    top_face = (lower_row == rows_dev * lat_devices - 1)[:, None]
    wide_courant = jnp.concatenate([from_west[stacked:, :, None], lon_courant], axis=2)
    tall_courant = jnp.concatenate([from_below[stacked:, None], lat_courant], axis=1)

    def increment_of(first, last):
        span = slice(first * level_count, last * level_count)
        wide_fields = jnp.concatenate(
            [from_west[span][:, :, None], flat_fields[span], from_east[span][:, :, None]], axis=2
        ).reshape(last - first, level_count, rows_dev, columns + 2)
        column_flux = face_flux(wide_courant, wide_fields[..., :-1], wide_fields[..., 1:])
        tall_fields = jnp.concatenate(
            [from_below[span][:, None], flat_fields[span], from_above[span][:, None]], axis=1
        ).reshape(last - first, level_count, rows_dev + 2, columns)
        row_flux = face_flux(tall_courant, tall_fields[:, :, :-1], tall_fields[:, :, 1:])
        row_flux = jnp.where(top_face, 0.0, row_flux)
        increment = -(column_flux[..., 1:] - column_flux[..., :-1]) - (
            row_flux[:, :, 1:] - row_flux[:, :, :-1]
        )
        return increment.reshape((last - first) * level_count, rows_dev, columns)

    half_rows = rows_dev // 2
    pair_shift = lat_devices // 2
    pair_perm = [(i, (i + pair_shift) % lat_devices) for i in range(lat_devices)]
    is_low = tile_index < pair_shift
    partner_index = (tile_index + pair_shift) % lat_devices

    def row_info(tile):
        row_global = tile * rows_dev + jnp.arange(rows_dev, dtype=jnp.int32)
        matched = filter_rows[None, :] == row_global[:, None]
        return jnp.any(matched, axis=1), jnp.sum(jnp.where(matched, cutoff[None, :], 0), axis=1)

    is_filtered, own_cut = row_info(tile_index)
    _, partner_cut = row_info(partner_index)
    row_cut = jnp.where(is_filtered, own_cut, partner_cut).astype(jnp.float32)
    kept_filtered = jnp.where(is_low, is_filtered[:half_rows], is_filtered[half_rows:])
    kept_cut = jnp.where(is_low, row_cut[:half_rows], row_cut[half_rows:])
    first_fields = field_count * 2 // 5
    field_spans = ((0, first_fields), (first_fields, field_count))
    outputs = []
    for first, last in field_spans:
        chunk_stack = (last - first) * level_count
        flat_increment = increment_of(first, last)
        low_half = flat_increment[:, :half_rows]
        high_half = flat_increment[:, half_rows:]
        kept = jnp.where(is_low, low_half, high_half)
        given = jnp.where(is_low, high_half, low_half)
        line_count = chunk_stack * half_rows // lon_devices
        line_index = lax.axis_index("lon") * line_count + jnp.arange(line_count, dtype=jnp.int32)
        line_cut = kept_cut[line_index % half_rows]
        taken = lax.ppermute(given, "lat", pair_perm)
        pair_lines = jnp.where(kept_filtered[None, :, None], kept, taken)
        full_lines = lax.all_to_all(
            pair_lines.reshape(chunk_stack * half_rows, columns),
            "lon",
            split_axis=0,
            concat_axis=1,
            tiled=True,
        )
        smoothed = filter_lines(full_lines, line_cut)
        returned = lax.all_to_all(
            smoothed, "lon", split_axis=1, concat_axis=0, tiled=True
        ).reshape(chunk_stack, half_rows, columns)
        handed_back = lax.ppermute(returned, "lat", pair_perm)
        smooth_rows = jnp.where(
            is_low,
            jnp.concatenate([returned, handed_back], axis=1),
            jnp.concatenate([handed_back, returned], axis=1),
        )
        final_increment = jnp.where(is_filtered[None, :, None], smooth_rows, flat_increment)
        outputs.append(flat_fields[first * level_count : last * level_count] + final_increment)
    return jnp.concatenate(outputs, axis=0).reshape(fields.shape)


def solution(mesh):
    placed = (P(None, None, "lat", "lon"), P(None, "lat", "lon"), P(None, "lat", "lon"), P(), P())
    return jax.shard_map(
        body, mesh=mesh, in_specs=placed, out_specs=P(None, None, "lat", "lon"), check_vma=False
    )
```

```python
from functools import partial
import math

import jax
import jax.numpy as jnp
from jax import lax
from jax.sharding import PartitionSpec as P

radix_len = 128


def phase_table(row_total, col_total, modulus):
    product = (
        jnp.arange(row_total, dtype=jnp.int32)[:, None]
        * jnp.arange(col_total, dtype=jnp.int32)[None, :]
        % modulus
    )
    angle = product.astype(jnp.float32) * (2.0 * math.pi / modulus)
    return (jnp.cos(angle), jnp.sin(angle))


def filter_lines(lines, line_cut):
    line_total, circle = lines.shape
    outer = circle // radix_len
    mixer = partial(jnp.einsum, precision=lax.Precision.HIGH)
    outer_cos, outer_sin = phase_table(outer, outer, outer)
    inner_cos, inner_sin = phase_table(radix_len, radix_len, radix_len)
    twist_cos, twist_sin = phase_table(outer, radix_len, circle)
    values = lines.reshape(line_total, outer, radix_len)
    first_re = mixer("lan,aj->ljn", values, outer_cos)
    first_im = -mixer("lan,aj->ljn", values, outer_sin)
    turned_re = first_re * twist_cos + first_im * twist_sin
    turned_im = first_im * twist_cos - first_re * twist_sin
    spec_re = mixer("ljn,nk->ljk", turned_re, inner_cos) + mixer(
        "ljn,nk->ljk", turned_im, inner_sin
    )
    spec_im = mixer("ljn,nk->ljk", turned_im, inner_cos) - mixer(
        "ljn,nk->ljk", turned_re, inner_sin
    )
    wave = (
        jnp.arange(outer, dtype=jnp.int32)[:, None]
        + outer * jnp.arange(radix_len, dtype=jnp.int32)[None, :]
    )
    mode_value = jnp.minimum(wave, circle - wave).astype(jnp.float32)[None]
    cut_value = line_cut[:, None, None]
    damp = jnp.where(mode_value <= cut_value, 1.0, (cut_value / jnp.maximum(mode_value, 1.0)) ** 2)
    spec_re = spec_re * damp
    spec_im = spec_im * damp
    back_re = mixer("ljk,kn->ljn", spec_re, inner_cos) - mixer("ljk,kn->ljn", spec_im, inner_sin)
    back_im = mixer("ljk,kn->ljn", spec_im, inner_cos) + mixer("ljk,kn->ljn", spec_re, inner_sin)
    untwist_re = back_re * twist_cos - back_im * twist_sin
    untwist_im = back_im * twist_cos + back_re * twist_sin
    result = mixer("ljn,ja->lan", untwist_re, outer_cos) - mixer(
        "ljn,ja->lan", untwist_im, outer_sin
    )
    return (result / circle).reshape(line_total, circle)


def face_flux(courant, near_value, far_value):
    return 0.5 * courant * (near_value + far_value) - 0.5 * courant * courant * (
        far_value - near_value
    )


def body(fields, lon_courant, lat_courant, filter_rows, cutoff):
    field_count, level_count, rows_dev, columns = fields.shape
    stacked = field_count * level_count
    lon_devices = lax.axis_size("lon")
    lat_devices = lax.axis_size("lat")
    flat_fields = fields.reshape(stacked, rows_dev, columns)
    eastward = [(i, (i + 1) % lon_devices) for i in range(lon_devices)]
    westward = [((i + 1) % lon_devices, i) for i in range(lon_devices)]
    northward = [(i, i + 1) for i in range(lat_devices - 1)]
    southward = [(i + 1, i) for i in range(lat_devices - 1)]
    from_west = lax.ppermute(
        jnp.concatenate([flat_fields[..., -1], lon_courant[..., -1]], axis=0), "lon", eastward
    )
    from_east = lax.ppermute(flat_fields[..., 0], "lon", westward)
    from_below = lax.ppermute(
        jnp.concatenate([flat_fields[:, -1], lat_courant[:, -1]], axis=0), "lat", northward
    )
    from_above = lax.ppermute(flat_fields[:, 0], "lat", southward)
    wide_fields = jnp.concatenate(
        [from_west[:stacked, :, None], flat_fields, from_east[:, :, None]], axis=2
    ).reshape(field_count, level_count, rows_dev, columns + 2)
    wide_courant = jnp.concatenate([from_west[stacked:, :, None], lon_courant], axis=2)
    column_flux = face_flux(wide_courant, wide_fields[..., :-1], wide_fields[..., 1:])
    tall_fields = jnp.concatenate(
        [from_below[:stacked, None], flat_fields, from_above[:, None]], axis=1
    ).reshape(field_count, level_count, rows_dev + 2, columns)
    tall_courant = jnp.concatenate([from_below[stacked:, None], lat_courant], axis=1)
    row_flux = face_flux(tall_courant, tall_fields[:, :, :-1], tall_fields[:, :, 1:])
    tile_index = lax.axis_index("lat")
    lower_row = tile_index * rows_dev - 1 + jnp.arange(rows_dev + 1, dtype=jnp.int32)
    row_flux = jnp.where((lower_row == rows_dev * lat_devices - 1)[:, None], 0.0, row_flux)
    increment = -(column_flux[..., 1:] - column_flux[..., :-1]) - (
        row_flux[:, :, 1:] - row_flux[:, :, :-1]
    )
    flat_increment = increment.reshape(stacked, rows_dev, columns)
    half_rows = rows_dev // 2
    pair_shift = lat_devices // 2
    pair_perm = [(i, (i + pair_shift) % lat_devices) for i in range(lat_devices)]
    is_low = tile_index < pair_shift
    partner_index = (tile_index + pair_shift) % lat_devices

    def row_info(tile):
        row_global = tile * rows_dev + jnp.arange(rows_dev, dtype=jnp.int32)
        matched = filter_rows[None, :] == row_global[:, None]
        return jnp.any(matched, axis=1), jnp.sum(jnp.where(matched, cutoff[None, :], 0), axis=1)

    is_filtered, own_cut = row_info(tile_index)
    _, partner_cut = row_info(partner_index)
    row_cut = jnp.where(is_filtered, own_cut, partner_cut).astype(jnp.float32)
    low_half = flat_increment[:, :half_rows]
    high_half = flat_increment[:, half_rows:]
    kept = jnp.where(is_low, low_half, high_half)
    given = jnp.where(is_low, high_half, low_half)
    kept_filtered = jnp.where(is_low, is_filtered[:half_rows], is_filtered[half_rows:])
    kept_cut = jnp.where(is_low, row_cut[:half_rows], row_cut[half_rows:])
    chunk_sizes = (stacked * 3 // 5, stacked - stacked * 3 // 5)
    returned_parts, handed_parts = [], []
    chunk_start = 0
    for chunk_stack in chunk_sizes:
        rows_of_part = slice(chunk_start, chunk_start + chunk_stack)
        chunk_start += chunk_stack
        line_count = chunk_stack * half_rows // lon_devices
        line_index = lax.axis_index("lon") * line_count + jnp.arange(line_count, dtype=jnp.int32)
        line_cut = kept_cut[line_index % half_rows]
        taken = lax.ppermute(given[rows_of_part], "lat", pair_perm)
        pair_lines = jnp.where(kept_filtered[None, :, None], kept[rows_of_part], taken)
        full_lines = lax.all_to_all(
            pair_lines.reshape(chunk_stack * half_rows, columns),
            "lon",
            split_axis=0,
            concat_axis=1,
            tiled=True,
        )
        smoothed = filter_lines(full_lines, line_cut)
        returned = lax.all_to_all(
            smoothed, "lon", split_axis=1, concat_axis=0, tiled=True
        ).reshape(chunk_stack, half_rows, columns)
        returned_parts.append(returned)
        handed_parts.append(lax.ppermute(returned, "lat", pair_perm))
    returned = jnp.concatenate(returned_parts, axis=0)
    handed_back = jnp.concatenate(handed_parts, axis=0)
    smooth_rows = jnp.where(
        is_low,
        jnp.concatenate([returned, handed_back], axis=1),
        jnp.concatenate([handed_back, returned], axis=1),
    )
    final_increment = jnp.where(is_filtered[None, :, None], smooth_rows, flat_increment)
    return (flat_fields + final_increment).reshape(fields.shape)


def solution(mesh):
    placed = (P(None, None, "lat", "lon"), P(None, "lat", "lon"), P(None, "lat", "lon"), P(), P())
    return jax.shard_map(
        body, mesh=mesh, in_specs=placed, out_specs=P(None, None, "lat", "lon"), check_vma=False
    )
```

```python
from functools import partial
import math

import jax
import jax.numpy as jnp
from jax import lax
from jax.sharding import PartitionSpec as P

radix_len = 128


def phase_table(row_total, col_total, modulus):
    product = (
        jnp.arange(row_total, dtype=jnp.int32)[:, None]
        * jnp.arange(col_total, dtype=jnp.int32)[None, :]
        % modulus
    )
    angle = product.astype(jnp.float32) * (2.0 * math.pi / modulus)
    return (jnp.cos(angle), jnp.sin(angle))


def filter_lines(lines, line_cut):
    line_total, circle = lines.shape
    outer = circle // radix_len
    mixer = partial(jnp.einsum, precision=lax.Precision.HIGH)
    outer_cos, outer_sin = phase_table(outer, outer, outer)
    inner_cos, inner_sin = phase_table(radix_len, radix_len, radix_len)
    twist_cos, twist_sin = phase_table(outer, radix_len, circle)
    values = lines.reshape(line_total, outer, radix_len)
    first_re = mixer("lan,aj->ljn", values, outer_cos)
    first_im = -mixer("lan,aj->ljn", values, outer_sin)
    turned_re = first_re * twist_cos + first_im * twist_sin
    turned_im = first_im * twist_cos - first_re * twist_sin
    spec_re = mixer("ljn,nk->ljk", turned_re, inner_cos) + mixer(
        "ljn,nk->ljk", turned_im, inner_sin
    )
    spec_im = mixer("ljn,nk->ljk", turned_im, inner_cos) - mixer(
        "ljn,nk->ljk", turned_re, inner_sin
    )
    wave = (
        jnp.arange(outer, dtype=jnp.int32)[:, None]
        + outer * jnp.arange(radix_len, dtype=jnp.int32)[None, :]
    )
    mode_value = jnp.minimum(wave, circle - wave).astype(jnp.float32)[None]
    cut_value = line_cut[:, None, None]
    damp = jnp.where(mode_value <= cut_value, 1.0, (cut_value / jnp.maximum(mode_value, 1.0)) ** 2)
    spec_re = spec_re * damp
    spec_im = spec_im * damp
    back_re = mixer("ljk,kn->ljn", spec_re, inner_cos) - mixer("ljk,kn->ljn", spec_im, inner_sin)
    back_im = mixer("ljk,kn->ljn", spec_im, inner_cos) + mixer("ljk,kn->ljn", spec_re, inner_sin)
    untwist_re = back_re * twist_cos - back_im * twist_sin
    untwist_im = back_im * twist_cos + back_re * twist_sin
    result = mixer("ljn,ja->lan", untwist_re, outer_cos) - mixer(
        "ljn,ja->lan", untwist_im, outer_sin
    )
    return (result / circle).reshape(line_total, circle)


def face_flux(courant, near_value, far_value):
    return 0.5 * courant * (near_value + far_value) - 0.5 * courant * courant * (
        far_value - near_value
    )


def body(fields, lon_courant, lat_courant, filter_rows, cutoff):
    field_count, level_count, rows_dev, columns = fields.shape
    stacked = field_count * level_count
    lon_devices = lax.axis_size("lon")
    lat_devices = lax.axis_size("lat")
    flat_fields = fields.reshape(stacked, rows_dev, columns)
    eastward = [(i, (i + 1) % lon_devices) for i in range(lon_devices)]
    westward = [((i + 1) % lon_devices, i) for i in range(lon_devices)]
    northward = [(i, i + 1) for i in range(lat_devices - 1)]
    southward = [(i + 1, i) for i in range(lat_devices - 1)]
    from_west = lax.ppermute(
        jnp.concatenate([flat_fields[..., -1], lon_courant[..., -1]], axis=0), "lon", eastward
    )
    from_east = lax.ppermute(flat_fields[..., 0], "lon", westward)
    from_below = lax.ppermute(
        jnp.concatenate([flat_fields[:, -1], lat_courant[:, -1]], axis=0), "lat", northward
    )
    from_above = lax.ppermute(flat_fields[:, 0], "lat", southward)
    wide_fields = jnp.concatenate(
        [from_west[:stacked, :, None], flat_fields, from_east[:, :, None]], axis=2
    ).reshape(field_count, level_count, rows_dev, columns + 2)
    wide_courant = jnp.concatenate([from_west[stacked:, :, None], lon_courant], axis=2)
    column_flux = face_flux(wide_courant, wide_fields[..., :-1], wide_fields[..., 1:])
    tall_fields = jnp.concatenate(
        [from_below[:stacked, None], flat_fields, from_above[:, None]], axis=1
    ).reshape(field_count, level_count, rows_dev + 2, columns)
    tall_courant = jnp.concatenate([from_below[stacked:, None], lat_courant], axis=1)
    row_flux = face_flux(tall_courant, tall_fields[:, :, :-1], tall_fields[:, :, 1:])
    tile_index = lax.axis_index("lat")
    lower_row = tile_index * rows_dev - 1 + jnp.arange(rows_dev + 1, dtype=jnp.int32)
    row_flux = jnp.where((lower_row == rows_dev * lat_devices - 1)[:, None], 0.0, row_flux)
    increment = -(column_flux[..., 1:] - column_flux[..., :-1]) - (
        row_flux[:, :, 1:] - row_flux[:, :, :-1]
    )
    flat_increment = increment.reshape(stacked, rows_dev, columns)
    half_rows = rows_dev // 2
    pair_shift = lat_devices // 2
    pair_perm = [(i, (i + pair_shift) % lat_devices) for i in range(lat_devices)]
    is_low = tile_index < pair_shift
    partner_index = (tile_index + pair_shift) % lat_devices

    def row_info(tile):
        row_global = tile * rows_dev + jnp.arange(rows_dev, dtype=jnp.int32)
        matched = filter_rows[None, :] == row_global[:, None]
        return jnp.any(matched, axis=1), jnp.sum(jnp.where(matched, cutoff[None, :], 0), axis=1)

    is_filtered, own_cut = row_info(tile_index)
    _, partner_cut = row_info(partner_index)
    row_cut = jnp.where(is_filtered, own_cut, partner_cut).astype(jnp.float32)
    low_half = flat_increment[:, :half_rows]
    high_half = flat_increment[:, half_rows:]
    kept = jnp.where(is_low, low_half, high_half)
    given = jnp.where(is_low, high_half, low_half)
    kept_filtered = jnp.where(is_low, is_filtered[:half_rows], is_filtered[half_rows:])
    kept_cut = jnp.where(is_low, row_cut[:half_rows], row_cut[half_rows:])
    chunk_sizes = (stacked // 5, stacked // 2, stacked - stacked // 5 - stacked // 2)
    returned_parts, handed_parts = [], []
    chunk_start = 0
    for chunk_stack in chunk_sizes:
        rows_of_part = slice(chunk_start, chunk_start + chunk_stack)
        chunk_start += chunk_stack
        line_count = chunk_stack * half_rows // lon_devices
        line_index = lax.axis_index("lon") * line_count + jnp.arange(line_count, dtype=jnp.int32)
        line_cut = kept_cut[line_index % half_rows]
        taken = lax.ppermute(given[rows_of_part], "lat", pair_perm)
        pair_lines = jnp.where(kept_filtered[None, :, None], kept[rows_of_part], taken)
        full_lines = lax.all_to_all(
            pair_lines.reshape(chunk_stack * half_rows, columns),
            "lon",
            split_axis=0,
            concat_axis=1,
            tiled=True,
        )
        smoothed = filter_lines(full_lines, line_cut)
        returned = lax.all_to_all(
            smoothed, "lon", split_axis=1, concat_axis=0, tiled=True
        ).reshape(chunk_stack, half_rows, columns)
        returned_parts.append(returned)
        handed_parts.append(lax.ppermute(returned, "lat", pair_perm))
    returned = jnp.concatenate(returned_parts, axis=0)
    handed_back = jnp.concatenate(handed_parts, axis=0)
    smooth_rows = jnp.where(
        is_low,
        jnp.concatenate([returned, handed_back], axis=1),
        jnp.concatenate([handed_back, returned], axis=1),
    )
    final_increment = jnp.where(is_filtered[None, :, None], smooth_rows, flat_increment)
    return (flat_fields + final_increment).reshape(fields.shape)


def solution(mesh):
    placed = (P(None, None, "lat", "lon"), P(None, "lat", "lon"), P(None, "lat", "lon"), P(), P())
    return jax.shard_map(
        body, mesh=mesh, in_specs=placed, out_specs=P(None, None, "lat", "lon"), check_vma=False
    )
```

```python
from functools import partial
import math

import jax
import jax.numpy as jnp
from jax import lax
from jax.sharding import PartitionSpec as P

radix_len = 128


def phase_table(row_total, col_total, modulus):
    product = (
        jnp.arange(row_total, dtype=jnp.int32)[:, None]
        * jnp.arange(col_total, dtype=jnp.int32)[None, :]
        % modulus
    )
    angle = product.astype(jnp.float32) * (2.0 * math.pi / modulus)
    return (jnp.cos(angle), jnp.sin(angle))


def filter_lines(lines, line_cut):
    line_total, circle = lines.shape
    outer = circle // radix_len
    mixer = partial(jnp.einsum, precision=lax.Precision.HIGH)
    outer_cos, outer_sin = phase_table(outer, outer, outer)
    inner_cos, inner_sin = phase_table(radix_len, radix_len, radix_len)
    twist_cos, twist_sin = phase_table(outer, radix_len, circle)
    values = lines.reshape(line_total, outer, radix_len)
    first_re = mixer("lan,aj->ljn", values, outer_cos)
    first_im = -mixer("lan,aj->ljn", values, outer_sin)
    turned_re = first_re * twist_cos + first_im * twist_sin
    turned_im = first_im * twist_cos - first_re * twist_sin
    spec_re = mixer("ljn,nk->ljk", turned_re, inner_cos) + mixer(
        "ljn,nk->ljk", turned_im, inner_sin
    )
    spec_im = mixer("ljn,nk->ljk", turned_im, inner_cos) - mixer(
        "ljn,nk->ljk", turned_re, inner_sin
    )
    wave = (
        jnp.arange(outer, dtype=jnp.int32)[:, None]
        + outer * jnp.arange(radix_len, dtype=jnp.int32)[None, :]
    )
    mode_value = jnp.minimum(wave, circle - wave).astype(jnp.float32)[None]
    cut_value = line_cut[:, None, None]
    damp = jnp.where(mode_value <= cut_value, 1.0, (cut_value / jnp.maximum(mode_value, 1.0)) ** 2)
    spec_re = spec_re * damp
    spec_im = spec_im * damp
    back_re = mixer("ljk,kn->ljn", spec_re, inner_cos) - mixer("ljk,kn->ljn", spec_im, inner_sin)
    back_im = mixer("ljk,kn->ljn", spec_im, inner_cos) + mixer("ljk,kn->ljn", spec_re, inner_sin)
    untwist_re = back_re * twist_cos - back_im * twist_sin
    untwist_im = back_im * twist_cos + back_re * twist_sin
    result = mixer("ljn,ja->lan", untwist_re, outer_cos) - mixer(
        "ljn,ja->lan", untwist_im, outer_sin
    )
    return (result / circle).reshape(line_total, circle)


def face_flux(courant, near_value, far_value):
    return 0.5 * courant * (near_value + far_value) - 0.5 * courant * courant * (
        far_value - near_value
    )


def body(fields, lon_courant, lat_courant, filter_rows, cutoff):
    field_count, level_count, rows_dev, columns = fields.shape
    stacked = field_count * level_count
    lon_devices = lax.axis_size("lon")
    lat_devices = lax.axis_size("lat")
    flat_fields = fields.reshape(stacked, rows_dev, columns)
    eastward = [(i, (i + 1) % lon_devices) for i in range(lon_devices)]
    westward = [((i + 1) % lon_devices, i) for i in range(lon_devices)]
    northward = [(i, i + 1) for i in range(lat_devices - 1)]
    southward = [(i + 1, i) for i in range(lat_devices - 1)]
    from_west = lax.ppermute(
        jnp.concatenate([flat_fields[..., -1], lon_courant[..., -1]], axis=0), "lon", eastward
    )
    from_east = lax.ppermute(flat_fields[..., 0], "lon", westward)
    from_below = lax.ppermute(
        jnp.concatenate([flat_fields[:, -1], lat_courant[:, -1]], axis=0), "lat", northward
    )
    from_above = lax.ppermute(flat_fields[:, 0], "lat", southward)
    tile_index = lax.axis_index("lat")
    lower_row = tile_index * rows_dev - 1 + jnp.arange(rows_dev + 1, dtype=jnp.int32)
    top_face = (lower_row == rows_dev * lat_devices - 1)[:, None]
    wide_courant = jnp.concatenate([from_west[stacked:, :, None], lon_courant], axis=2)
    tall_courant = jnp.concatenate([from_below[stacked:, None], lat_courant], axis=1)

    def increment_of(first, last):
        span = slice(first * level_count, last * level_count)
        wide_fields = jnp.concatenate(
            [from_west[span][:, :, None], flat_fields[span], from_east[span][:, :, None]], axis=2
        ).reshape(last - first, level_count, rows_dev, columns + 2)
        column_flux = face_flux(wide_courant, wide_fields[..., :-1], wide_fields[..., 1:])
        tall_fields = jnp.concatenate(
            [from_below[span][:, None], flat_fields[span], from_above[span][:, None]], axis=1
        ).reshape(last - first, level_count, rows_dev + 2, columns)
        row_flux = face_flux(tall_courant, tall_fields[:, :, :-1], tall_fields[:, :, 1:])
        row_flux = jnp.where(top_face, 0.0, row_flux)
        increment = -(column_flux[..., 1:] - column_flux[..., :-1]) - (
            row_flux[:, :, 1:] - row_flux[:, :, :-1]
        )
        return increment.reshape((last - first) * level_count, rows_dev, columns)

    half_rows = rows_dev // 2
    pair_shift = lat_devices // 2
    pair_perm = [(i, (i + pair_shift) % lat_devices) for i in range(lat_devices)]
    is_low = tile_index < pair_shift
    partner_index = (tile_index + pair_shift) % lat_devices

    def row_info(tile):
        row_global = tile * rows_dev + jnp.arange(rows_dev, dtype=jnp.int32)
        matched = filter_rows[None, :] == row_global[:, None]
        return jnp.any(matched, axis=1), jnp.sum(jnp.where(matched, cutoff[None, :], 0), axis=1)

    is_filtered, own_cut = row_info(tile_index)
    _, partner_cut = row_info(partner_index)
    row_cut = jnp.where(is_filtered, own_cut, partner_cut).astype(jnp.float32)
    kept_filtered = jnp.where(is_low, is_filtered[:half_rows], is_filtered[half_rows:])
    kept_cut = jnp.where(is_low, row_cut[:half_rows], row_cut[half_rows:])
    first_fields = field_count * 3 // 5
    field_spans = ((0, first_fields), (first_fields, field_count))
    outputs = []
    for first, last in field_spans:
        chunk_stack = (last - first) * level_count
        flat_increment = increment_of(first, last)
        low_half = flat_increment[:, :half_rows]
        high_half = flat_increment[:, half_rows:]
        kept = jnp.where(is_low, low_half, high_half)
        given = jnp.where(is_low, high_half, low_half)
        line_count = chunk_stack * half_rows // lon_devices
        line_index = lax.axis_index("lon") * line_count + jnp.arange(line_count, dtype=jnp.int32)
        line_cut = kept_cut[line_index % half_rows]
        taken = lax.ppermute(given, "lat", pair_perm)
        pair_lines = jnp.where(kept_filtered[None, :, None], kept, taken)
        full_lines = lax.all_to_all(
            pair_lines.reshape(chunk_stack * half_rows, columns),
            "lon",
            split_axis=0,
            concat_axis=1,
            tiled=True,
        )
        smoothed = filter_lines(full_lines, line_cut)
        returned = lax.all_to_all(
            smoothed, "lon", split_axis=1, concat_axis=0, tiled=True
        ).reshape(chunk_stack, half_rows, columns)
        handed_back = lax.ppermute(returned, "lat", pair_perm)
        smooth_rows = jnp.where(
            is_low,
            jnp.concatenate([returned, handed_back], axis=1),
            jnp.concatenate([handed_back, returned], axis=1),
        )
        final_increment = jnp.where(is_filtered[None, :, None], smooth_rows, flat_increment)
        outputs.append(flat_fields[first * level_count : last * level_count] + final_increment)
    return jnp.concatenate(outputs, axis=0).reshape(fields.shape)


def solution(mesh):
    placed = (P(None, None, "lat", "lon"), P(None, "lat", "lon"), P(None, "lat", "lon"), P(), P())
    return jax.shard_map(
        body, mesh=mesh, in_specs=placed, out_specs=P(None, None, "lat", "lon"), check_vma=False
    )
```

```python
from functools import partial
import math

import jax
import jax.numpy as jnp
from jax import lax
from jax.sharding import PartitionSpec as P

radix_len = 128


def phase_table(row_total, col_total, modulus):
    product = (
        jnp.arange(row_total, dtype=jnp.int32)[:, None]
        * jnp.arange(col_total, dtype=jnp.int32)[None, :]
        % modulus
    )
    angle = product.astype(jnp.float32) * (2.0 * math.pi / modulus)
    return (jnp.cos(angle), jnp.sin(angle))


def filter_lines(lines, line_cut):
    line_total, circle = lines.shape
    outer = circle // radix_len
    mixer = partial(jnp.einsum, precision=lax.Precision.HIGH)
    outer_cos, outer_sin = phase_table(outer, outer, outer)
    inner_cos, inner_sin = phase_table(radix_len, radix_len, radix_len)
    twist_cos, twist_sin = phase_table(outer, radix_len, circle)
    values = lines.reshape(line_total, outer, radix_len)
    first_re = mixer("lan,aj->ljn", values, outer_cos)
    first_im = -mixer("lan,aj->ljn", values, outer_sin)
    turned_re = first_re * twist_cos + first_im * twist_sin
    turned_im = first_im * twist_cos - first_re * twist_sin
    spec_re = mixer("ljn,nk->ljk", turned_re, inner_cos) + mixer(
        "ljn,nk->ljk", turned_im, inner_sin
    )
    spec_im = mixer("ljn,nk->ljk", turned_im, inner_cos) - mixer(
        "ljn,nk->ljk", turned_re, inner_sin
    )
    wave = (
        jnp.arange(outer, dtype=jnp.int32)[:, None]
        + outer * jnp.arange(radix_len, dtype=jnp.int32)[None, :]
    )
    mode_value = jnp.minimum(wave, circle - wave).astype(jnp.float32)[None]
    cut_value = line_cut[:, None, None]
    damp = jnp.where(mode_value <= cut_value, 1.0, (cut_value / jnp.maximum(mode_value, 1.0)) ** 2)
    spec_re = spec_re * damp
    spec_im = spec_im * damp
    back_re = mixer("ljk,kn->ljn", spec_re, inner_cos) - mixer("ljk,kn->ljn", spec_im, inner_sin)
    back_im = mixer("ljk,kn->ljn", spec_im, inner_cos) + mixer("ljk,kn->ljn", spec_re, inner_sin)
    untwist_re = back_re * twist_cos - back_im * twist_sin
    untwist_im = back_im * twist_cos + back_re * twist_sin
    result = mixer("ljn,ja->lan", untwist_re, outer_cos) - mixer(
        "ljn,ja->lan", untwist_im, outer_sin
    )
    return (result / circle).reshape(line_total, circle)


def face_flux(courant, near_value, far_value):
    return 0.5 * courant * (near_value + far_value) - 0.5 * courant * courant * (
        far_value - near_value
    )


def body(fields, lon_courant, lat_courant, filter_rows, cutoff):
    field_count, level_count, rows_dev, columns = fields.shape
    stacked = field_count * level_count
    lon_devices = lax.axis_size("lon")
    lat_devices = lax.axis_size("lat")
    flat_fields = fields.reshape(stacked, rows_dev, columns)
    eastward = [(i, (i + 1) % lon_devices) for i in range(lon_devices)]
    westward = [((i + 1) % lon_devices, i) for i in range(lon_devices)]
    northward = [(i, i + 1) for i in range(lat_devices - 1)]
    southward = [(i + 1, i) for i in range(lat_devices - 1)]
    from_west = lax.ppermute(
        jnp.concatenate([flat_fields[..., -1], lon_courant[..., -1]], axis=0), "lon", eastward
    )
    from_east = lax.ppermute(flat_fields[..., 0], "lon", westward)
    from_below = lax.ppermute(
        jnp.concatenate([flat_fields[:, -1], lat_courant[:, -1]], axis=0), "lat", northward
    )
    from_above = lax.ppermute(flat_fields[:, 0], "lat", southward)
    wide_fields = jnp.concatenate(
        [from_west[:stacked, :, None], flat_fields, from_east[:, :, None]], axis=2
    ).reshape(field_count, level_count, rows_dev, columns + 2)
    wide_courant = jnp.concatenate([from_west[stacked:, :, None], lon_courant], axis=2)
    column_flux = face_flux(wide_courant, wide_fields[..., :-1], wide_fields[..., 1:])
    tall_fields = jnp.concatenate(
        [from_below[:stacked, None], flat_fields, from_above[:, None]], axis=1
    ).reshape(field_count, level_count, rows_dev + 2, columns)
    tall_courant = jnp.concatenate([from_below[stacked:, None], lat_courant], axis=1)
    row_flux = face_flux(tall_courant, tall_fields[:, :, :-1], tall_fields[:, :, 1:])
    tile_index = lax.axis_index("lat")
    lower_row = tile_index * rows_dev - 1 + jnp.arange(rows_dev + 1, dtype=jnp.int32)
    row_flux = jnp.where((lower_row == rows_dev * lat_devices - 1)[:, None], 0.0, row_flux)
    increment = -(column_flux[..., 1:] - column_flux[..., :-1]) - (
        row_flux[:, :, 1:] - row_flux[:, :, :-1]
    )
    flat_increment = increment.reshape(stacked, rows_dev, columns)
    half_rows = rows_dev // 2
    pair_shift = lat_devices // 2
    pair_perm = [(i, (i + pair_shift) % lat_devices) for i in range(lat_devices)]
    is_low = tile_index < pair_shift
    partner_index = (tile_index + pair_shift) % lat_devices

    def row_info(tile):
        row_global = tile * rows_dev + jnp.arange(rows_dev, dtype=jnp.int32)
        matched = filter_rows[None, :] == row_global[:, None]
        return jnp.any(matched, axis=1), jnp.sum(jnp.where(matched, cutoff[None, :], 0), axis=1)

    is_filtered, own_cut = row_info(tile_index)
    _, partner_cut = row_info(partner_index)
    row_cut = jnp.where(is_filtered, own_cut, partner_cut).astype(jnp.float32)
    low_half = flat_increment[:, :half_rows]
    high_half = flat_increment[:, half_rows:]
    kept = jnp.where(is_low, low_half, high_half)
    given = jnp.where(is_low, high_half, low_half)
    kept_filtered = jnp.where(is_low, is_filtered[:half_rows], is_filtered[half_rows:])
    kept_cut = jnp.where(is_low, row_cut[:half_rows], row_cut[half_rows:])
    chunk_sizes = (stacked * 2 // 5, stacked - stacked * 2 // 5)
    returned_parts, handed_parts = [], []
    chunk_start = 0
    for chunk_stack in chunk_sizes:
        rows_of_part = slice(chunk_start, chunk_start + chunk_stack)
        chunk_start += chunk_stack
        line_count = chunk_stack * half_rows // lon_devices
        lon_index = lax.axis_index("lon")
        line_index = lon_index * line_count + jnp.arange(line_count, dtype=jnp.int32)
        line_cut = kept_cut[line_index % half_rows]
        taken = lax.ppermute(given[rows_of_part], "lat", pair_perm)
        pair_lines = jnp.where(kept_filtered[None, :, None], kept[rows_of_part], taken)
        blocks = pair_lines.reshape(lon_devices, line_count, columns)
        shift_order = (lon_index - jnp.arange(lon_devices, dtype=jnp.int32)) % lon_devices
        outgoing = jnp.take(blocks, shift_order, axis=0)
        pieces = [outgoing[0]]
        for shift in range(1, lon_devices):
            toward = [(i, (i - shift) % lon_devices) for i in range(lon_devices)]
            pieces.append(lax.ppermute(outgoing[shift], "lon", toward))
        rotated_lines = jnp.concatenate(pieces, axis=1)
        smoothed = filter_lines(rotated_lines, line_cut)
        coming = [smoothed[:, :columns]]
        for shift in range(1, lon_devices):
            toward = [(i, (i + shift) % lon_devices) for i in range(lon_devices)]
            coming.append(
                lax.ppermute(smoothed[:, shift * columns : (shift + 1) * columns], "lon", toward)
            )
        returned = jnp.take(jnp.stack(coming), shift_order, axis=0).reshape(
            chunk_stack, half_rows, columns
        )
        returned_parts.append(returned)
        handed_parts.append(lax.ppermute(returned, "lat", pair_perm))
    returned = jnp.concatenate(returned_parts, axis=0)
    handed_back = jnp.concatenate(handed_parts, axis=0)
    smooth_rows = jnp.where(
        is_low,
        jnp.concatenate([returned, handed_back], axis=1),
        jnp.concatenate([handed_back, returned], axis=1),
    )
    final_increment = jnp.where(is_filtered[None, :, None], smooth_rows, flat_increment)
    return (flat_fields + final_increment).reshape(fields.shape)


def solution(mesh):
    placed = (P(None, None, "lat", "lon"), P(None, "lat", "lon"), P(None, "lat", "lon"), P(), P())
    return jax.shard_map(
        body, mesh=mesh, in_specs=placed, out_specs=P(None, None, "lat", "lon"), check_vma=False
    )
```

```python
from functools import partial
import math

import jax
import jax.numpy as jnp
from jax import lax
from jax.sharding import PartitionSpec as P

radix_len = 128


def phase_table(row_total, col_total, modulus):
    product = (
        jnp.arange(row_total, dtype=jnp.int32)[:, None]
        * jnp.arange(col_total, dtype=jnp.int32)[None, :]
        % modulus
    )
    angle = product.astype(jnp.float32) * (2.0 * math.pi / modulus)
    return (jnp.cos(angle), jnp.sin(angle))


def filter_lines(lines, line_cut):
    line_total, circle = lines.shape
    outer = circle // radix_len
    mixer = partial(jnp.einsum, precision=lax.Precision.HIGH)
    outer_cos, outer_sin = phase_table(outer, outer, outer)
    inner_cos, inner_sin = phase_table(radix_len, radix_len, radix_len)
    twist_cos, twist_sin = phase_table(outer, radix_len, circle)
    values = lines.reshape(line_total, outer, radix_len)
    first_re = mixer("lan,aj->ljn", values, outer_cos)
    first_im = -mixer("lan,aj->ljn", values, outer_sin)
    turned_re = first_re * twist_cos + first_im * twist_sin
    turned_im = first_im * twist_cos - first_re * twist_sin
    spec_re = mixer("ljn,nk->ljk", turned_re, inner_cos) + mixer(
        "ljn,nk->ljk", turned_im, inner_sin
    )
    spec_im = mixer("ljn,nk->ljk", turned_im, inner_cos) - mixer(
        "ljn,nk->ljk", turned_re, inner_sin
    )
    wave = (
        jnp.arange(outer, dtype=jnp.int32)[:, None]
        + outer * jnp.arange(radix_len, dtype=jnp.int32)[None, :]
    )
    mode_value = jnp.minimum(wave, circle - wave).astype(jnp.float32)[None]
    cut_value = line_cut[:, None, None]
    damp = jnp.where(mode_value <= cut_value, 1.0, (cut_value / jnp.maximum(mode_value, 1.0)) ** 2)
    spec_re = spec_re * damp
    spec_im = spec_im * damp
    back_re = mixer("ljk,kn->ljn", spec_re, inner_cos) - mixer("ljk,kn->ljn", spec_im, inner_sin)
    back_im = mixer("ljk,kn->ljn", spec_im, inner_cos) + mixer("ljk,kn->ljn", spec_re, inner_sin)
    untwist_re = back_re * twist_cos - back_im * twist_sin
    untwist_im = back_im * twist_cos + back_re * twist_sin
    result = mixer("ljn,ja->lan", untwist_re, outer_cos) - mixer(
        "ljn,ja->lan", untwist_im, outer_sin
    )
    return (result / circle).reshape(line_total, circle)


def face_flux(courant, near_value, far_value):
    return 0.5 * courant * (near_value + far_value) - 0.5 * courant * courant * (
        far_value - near_value
    )


def body(fields, lon_courant, lat_courant, filter_rows, cutoff):
    field_count, level_count, rows_dev, columns = fields.shape
    stacked = field_count * level_count
    lon_devices = lax.axis_size("lon")
    lat_devices = lax.axis_size("lat")
    flat_fields = fields.reshape(stacked, rows_dev, columns)
    eastward = [(i, (i + 1) % lon_devices) for i in range(lon_devices)]
    westward = [((i + 1) % lon_devices, i) for i in range(lon_devices)]
    northward = [(i, i + 1) for i in range(lat_devices - 1)]
    southward = [(i + 1, i) for i in range(lat_devices - 1)]
    from_west = lax.ppermute(
        jnp.concatenate([flat_fields[..., -1], lon_courant[..., -1]], axis=0), "lon", eastward
    )
    from_east = lax.ppermute(flat_fields[..., 0], "lon", westward)
    from_below = lax.ppermute(
        jnp.concatenate([flat_fields[:, -1], lat_courant[:, -1]], axis=0), "lat", northward
    )
    from_above = lax.ppermute(flat_fields[:, 0], "lat", southward)
    wide_fields = jnp.concatenate(
        [from_west[:stacked, :, None], flat_fields, from_east[:, :, None]], axis=2
    ).reshape(field_count, level_count, rows_dev, columns + 2)
    wide_courant = jnp.concatenate([from_west[stacked:, :, None], lon_courant], axis=2)
    column_flux = face_flux(wide_courant, wide_fields[..., :-1], wide_fields[..., 1:])
    tile_index = lax.axis_index("lat")
    above_fields = from_above.reshape(field_count, level_count, 1, columns)
    upper = jnp.concatenate([fields[:, :, 1:], above_fields], axis=2)
    north_flux = face_flux(lat_courant, fields, upper)
    own_row = tile_index * rows_dev + jnp.arange(rows_dev, dtype=jnp.int32)
    north_flux = jnp.where((own_row == rows_dev * lat_devices - 1)[:, None], 0.0, north_flux)
    south_edge = face_flux(
        from_below[stacked:],
        from_below[:stacked].reshape(field_count, level_count, columns),
        fields[:, :, 0],
    )
    south_flux = jnp.concatenate([south_edge[:, :, None], north_flux[:, :, :-1]], axis=2)
    increment = -(column_flux[..., 1:] - column_flux[..., :-1]) - (north_flux - south_flux)
    flat_increment = increment.reshape(stacked, rows_dev, columns)
    half_rows = rows_dev // 2
    pair_shift = lat_devices // 2
    pair_perm = [(i, (i + pair_shift) % lat_devices) for i in range(lat_devices)]
    is_low = tile_index < pair_shift
    partner_index = (tile_index + pair_shift) % lat_devices

    def row_info(tile):
        row_global = tile * rows_dev + jnp.arange(rows_dev, dtype=jnp.int32)
        matched = filter_rows[None, :] == row_global[:, None]
        return jnp.any(matched, axis=1), jnp.sum(jnp.where(matched, cutoff[None, :], 0), axis=1)

    is_filtered, own_cut = row_info(tile_index)
    _, partner_cut = row_info(partner_index)
    row_cut = jnp.where(is_filtered, own_cut, partner_cut).astype(jnp.float32)
    low_half = flat_increment[:, :half_rows]
    high_half = flat_increment[:, half_rows:]
    kept = jnp.where(is_low, low_half, high_half)
    given = jnp.where(is_low, high_half, low_half)
    kept_filtered = jnp.where(is_low, is_filtered[:half_rows], is_filtered[half_rows:])
    kept_cut = jnp.where(is_low, row_cut[:half_rows], row_cut[half_rows:])
    chunk_sizes = (stacked * 2 // 5, stacked - stacked * 2 // 5)
    returned_parts, handed_parts = [], []
    chunk_start = 0
    for chunk_stack in chunk_sizes:
        rows_of_part = slice(chunk_start, chunk_start + chunk_stack)
        chunk_start += chunk_stack
        line_count = chunk_stack * half_rows // lon_devices
        line_index = lax.axis_index("lon") * line_count + jnp.arange(line_count, dtype=jnp.int32)
        line_cut = kept_cut[line_index % half_rows]
        taken = lax.ppermute(given[rows_of_part], "lat", pair_perm)
        pair_lines = jnp.where(kept_filtered[None, :, None], kept[rows_of_part], taken)
        full_lines = lax.all_to_all(
            pair_lines.reshape(chunk_stack * half_rows, columns),
            "lon",
            split_axis=0,
            concat_axis=1,
            tiled=True,
        )
        smoothed = filter_lines(full_lines, line_cut)
        returned = lax.all_to_all(
            smoothed, "lon", split_axis=1, concat_axis=0, tiled=True
        ).reshape(chunk_stack, half_rows, columns)
        returned_parts.append(returned)
        handed_parts.append(lax.ppermute(returned, "lat", pair_perm))
    returned = jnp.concatenate(returned_parts, axis=0)
    handed_back = jnp.concatenate(handed_parts, axis=0)
    smooth_rows = jnp.where(
        is_low,
        jnp.concatenate([returned, handed_back], axis=1),
        jnp.concatenate([handed_back, returned], axis=1),
    )
    final_increment = jnp.where(is_filtered[None, :, None], smooth_rows, flat_increment)
    return (flat_fields + final_increment).reshape(fields.shape)


def solution(mesh):
    placed = (P(None, None, "lat", "lon"), P(None, "lat", "lon"), P(None, "lat", "lon"), P(), P())
    return jax.shard_map(
        body, mesh=mesh, in_specs=placed, out_specs=P(None, None, "lat", "lon"), check_vma=False
    )
```

```python
from functools import partial
import math

import jax
import jax.numpy as jnp
from jax import lax
from jax.sharding import PartitionSpec as P

radix_len = 128


def phase_table(row_total, col_total, modulus):
    product = (
        jnp.arange(row_total, dtype=jnp.int32)[:, None]
        * jnp.arange(col_total, dtype=jnp.int32)[None, :]
        % modulus
    )
    angle = product.astype(jnp.float32) * (2.0 * math.pi / modulus)
    return (jnp.cos(angle), jnp.sin(angle))


def filter_lines(lines, line_cut):
    line_total, circle = lines.shape
    outer = circle // radix_len
    mixer = partial(jnp.einsum, precision=lax.Precision.HIGH)
    outer_cos, outer_sin = phase_table(outer, outer, outer)
    inner_cos, inner_sin = phase_table(radix_len, radix_len, radix_len)
    twist_cos, twist_sin = phase_table(outer, radix_len, circle)
    values = lines.reshape(line_total, outer, radix_len)
    first_re = mixer("lan,aj->ljn", values, outer_cos)
    first_im = -mixer("lan,aj->ljn", values, outer_sin)
    turned_re = first_re * twist_cos + first_im * twist_sin
    turned_im = first_im * twist_cos - first_re * twist_sin
    spec_re = mixer("ljn,nk->ljk", turned_re, inner_cos) + mixer(
        "ljn,nk->ljk", turned_im, inner_sin
    )
    spec_im = mixer("ljn,nk->ljk", turned_im, inner_cos) - mixer(
        "ljn,nk->ljk", turned_re, inner_sin
    )
    wave = (
        jnp.arange(outer, dtype=jnp.int32)[:, None]
        + outer * jnp.arange(radix_len, dtype=jnp.int32)[None, :]
    )
    mode_value = jnp.minimum(wave, circle - wave).astype(jnp.float32)[None]
    cut_value = line_cut[:, None, None]
    damp = jnp.where(mode_value <= cut_value, 1.0, (cut_value / jnp.maximum(mode_value, 1.0)) ** 2)
    spec_re = spec_re * damp
    spec_im = spec_im * damp
    back_re = mixer("ljk,kn->ljn", spec_re, inner_cos) - mixer("ljk,kn->ljn", spec_im, inner_sin)
    back_im = mixer("ljk,kn->ljn", spec_im, inner_cos) + mixer("ljk,kn->ljn", spec_re, inner_sin)
    untwist_re = back_re * twist_cos - back_im * twist_sin
    untwist_im = back_im * twist_cos + back_re * twist_sin
    result = mixer("ljn,ja->lan", untwist_re, outer_cos) - mixer(
        "ljn,ja->lan", untwist_im, outer_sin
    )
    return (result / circle).reshape(line_total, circle)


def face_flux(courant, near_value, far_value):
    return 0.5 * courant * (near_value + far_value) - 0.5 * courant * courant * (
        far_value - near_value
    )


def body(fields, lon_courant, lat_courant, filter_rows, cutoff):
    field_count, level_count, rows_dev, columns = fields.shape
    stacked = field_count * level_count
    lon_devices = lax.axis_size("lon")
    lat_devices = lax.axis_size("lat")
    flat_fields = fields.reshape(stacked, rows_dev, columns)
    eastward = [(i, (i + 1) % lon_devices) for i in range(lon_devices)]
    westward = [((i + 1) % lon_devices, i) for i in range(lon_devices)]
    northward = [(i, i + 1) for i in range(lat_devices - 1)]
    southward = [(i + 1, i) for i in range(lat_devices - 1)]
    from_west = lax.ppermute(
        jnp.concatenate([fields[..., -1], lon_courant[None, ..., -1]], axis=0), "lon", eastward
    )
    from_east = lax.ppermute(fields[..., 0], "lon", westward)
    from_below = lax.ppermute(
        jnp.concatenate([fields[:, :, -1], lat_courant[None, :, -1]], axis=0), "lat", northward
    )
    from_above = lax.ppermute(fields[:, :, 0], "lat", southward)
    wide_fields = jnp.concatenate(
        [from_west[:field_count, ..., None], fields, from_east[..., None]], axis=3
    )
    wide_courant = jnp.concatenate([from_west[field_count, ..., None], lon_courant], axis=2)
    column_flux = face_flux(wide_courant, wide_fields[..., :-1], wide_fields[..., 1:])
    tall_fields = jnp.concatenate(
        [from_below[:field_count, :, None], fields, from_above[:, :, None]], axis=2
    )
    tall_courant = jnp.concatenate([from_below[field_count, :, None], lat_courant], axis=1)
    row_flux = face_flux(tall_courant, tall_fields[:, :, :-1], tall_fields[:, :, 1:])
    tile_index = lax.axis_index("lat")
    lower_row = tile_index * rows_dev - 1 + jnp.arange(rows_dev + 1, dtype=jnp.int32)
    row_flux = jnp.where((lower_row == rows_dev * lat_devices - 1)[:, None], 0.0, row_flux)
    increment = -(column_flux[..., 1:] - column_flux[..., :-1]) - (
        row_flux[:, :, 1:] - row_flux[:, :, :-1]
    )
    flat_increment = increment.reshape(stacked, rows_dev, columns)
    half_rows = rows_dev // 2
    pair_shift = lat_devices // 2
    pair_perm = [(i, (i + pair_shift) % lat_devices) for i in range(lat_devices)]
    is_low = tile_index < pair_shift
    partner_index = (tile_index + pair_shift) % lat_devices

    def row_info(tile):
        row_global = tile * rows_dev + jnp.arange(rows_dev, dtype=jnp.int32)
        matched = filter_rows[None, :] == row_global[:, None]
        return jnp.any(matched, axis=1), jnp.sum(jnp.where(matched, cutoff[None, :], 0), axis=1)

    is_filtered, own_cut = row_info(tile_index)
    _, partner_cut = row_info(partner_index)
    row_cut = jnp.where(is_filtered, own_cut, partner_cut).astype(jnp.float32)
    low_half = flat_increment[:, :half_rows]
    high_half = flat_increment[:, half_rows:]
    kept = jnp.where(is_low, low_half, high_half)
    given = jnp.where(is_low, high_half, low_half)
    kept_filtered = jnp.where(is_low, is_filtered[:half_rows], is_filtered[half_rows:])
    kept_cut = jnp.where(is_low, row_cut[:half_rows], row_cut[half_rows:])
    chunk_sizes = (stacked * 2 // 5, stacked - stacked * 2 // 5)
    returned_parts, handed_parts = [], []
    chunk_start = 0
    for chunk_stack in chunk_sizes:
        rows_of_part = slice(chunk_start, chunk_start + chunk_stack)
        chunk_start += chunk_stack
        line_count = chunk_stack * half_rows // lon_devices
        line_index = lax.axis_index("lon") * line_count + jnp.arange(line_count, dtype=jnp.int32)
        line_cut = kept_cut[line_index % half_rows]
        taken = lax.ppermute(given[rows_of_part], "lat", pair_perm)
        pair_lines = jnp.where(kept_filtered[None, :, None], kept[rows_of_part], taken)
        full_lines = lax.all_to_all(
            pair_lines.reshape(chunk_stack * half_rows, columns),
            "lon",
            split_axis=0,
            concat_axis=1,
            tiled=True,
        )
        smoothed = filter_lines(full_lines, line_cut)
        returned = lax.all_to_all(
            smoothed, "lon", split_axis=1, concat_axis=0, tiled=True
        ).reshape(chunk_stack, half_rows, columns)
        returned_parts.append(returned)
        handed_parts.append(lax.ppermute(returned, "lat", pair_perm))
    returned = jnp.concatenate(returned_parts, axis=0)
    handed_back = jnp.concatenate(handed_parts, axis=0)
    smooth_rows = jnp.where(
        is_low,
        jnp.concatenate([returned, handed_back], axis=1),
        jnp.concatenate([handed_back, returned], axis=1),
    )
    final_increment = jnp.where(is_filtered[None, :, None], smooth_rows, flat_increment)
    return (flat_fields + final_increment).reshape(fields.shape)


def solution(mesh):
    placed = (P(None, None, "lat", "lon"), P(None, "lat", "lon"), P(None, "lat", "lon"), P(), P())
    return jax.shard_map(
        body, mesh=mesh, in_specs=placed, out_specs=P(None, None, "lat", "lon"), check_vma=False
    )
```

```python
from functools import partial
import math

import jax
import jax.numpy as jnp
from jax import lax
from jax.sharding import PartitionSpec as P

radix_len = 128


def phase_table(row_total, col_total, modulus):
    product = (
        jnp.arange(row_total, dtype=jnp.int32)[:, None]
        * jnp.arange(col_total, dtype=jnp.int32)[None, :]
        % modulus
    )
    angle = product.astype(jnp.float32) * (2.0 * math.pi / modulus)
    return (jnp.cos(angle), jnp.sin(angle))


def filter_lines(lines, line_cut):
    line_total, circle = lines.shape
    outer = circle // radix_len
    mixer = partial(jnp.einsum, precision=lax.Precision.HIGH)
    outer_cos, outer_sin = phase_table(outer, outer, outer)
    inner_cos, inner_sin = phase_table(radix_len, radix_len, radix_len)
    twist_cos, twist_sin = phase_table(outer, radix_len, circle)
    values = lines.reshape(line_total, outer, radix_len)
    first_re = mixer("lan,aj->ljn", values, outer_cos)
    first_im = -mixer("lan,aj->ljn", values, outer_sin)
    turned_re = first_re * twist_cos + first_im * twist_sin
    turned_im = first_im * twist_cos - first_re * twist_sin
    spec_re = mixer("ljn,nk->ljk", turned_re, inner_cos) + mixer(
        "ljn,nk->ljk", turned_im, inner_sin
    )
    spec_im = mixer("ljn,nk->ljk", turned_im, inner_cos) - mixer(
        "ljn,nk->ljk", turned_re, inner_sin
    )
    wave = (
        jnp.arange(outer, dtype=jnp.int32)[:, None]
        + outer * jnp.arange(radix_len, dtype=jnp.int32)[None, :]
    )
    mode_value = jnp.minimum(wave, circle - wave).astype(jnp.float32)[None]
    cut_value = line_cut[:, None, None]
    damp = jnp.where(mode_value <= cut_value, 1.0, (cut_value / jnp.maximum(mode_value, 1.0)) ** 2)
    spec_re = spec_re * damp
    spec_im = spec_im * damp
    back_re = mixer("ljk,kn->ljn", spec_re, inner_cos) - mixer("ljk,kn->ljn", spec_im, inner_sin)
    back_im = mixer("ljk,kn->ljn", spec_im, inner_cos) + mixer("ljk,kn->ljn", spec_re, inner_sin)
    untwist_re = back_re * twist_cos - back_im * twist_sin
    untwist_im = back_im * twist_cos + back_re * twist_sin
    result = mixer("ljn,ja->lan", untwist_re, outer_cos) - mixer(
        "ljn,ja->lan", untwist_im, outer_sin
    )
    return (result / circle).reshape(line_total, circle)


def face_flux(courant, near_value, far_value):
    return 0.5 * courant * (near_value + far_value) - 0.5 * courant * courant * (
        far_value - near_value
    )


def body(fields, lon_courant, lat_courant, filter_rows, cutoff):
    field_count, level_count, rows_dev, columns = fields.shape
    stacked = field_count * level_count
    lon_devices = lax.axis_size("lon")
    lat_devices = lax.axis_size("lat")
    flat_fields = fields.reshape(stacked, rows_dev, columns)
    eastward = [(i, (i + 1) % lon_devices) for i in range(lon_devices)]
    westward = [((i + 1) % lon_devices, i) for i in range(lon_devices)]
    northward = [(i, i + 1) for i in range(lat_devices - 1)]
    southward = [(i + 1, i) for i in range(lat_devices - 1)]
    from_west = lax.ppermute(
        jnp.concatenate([flat_fields[..., -1], lon_courant[..., -1]], axis=0), "lon", eastward
    )
    from_east = lax.ppermute(flat_fields[..., 0], "lon", westward)
    from_below = lax.ppermute(
        jnp.concatenate([flat_fields[:, -1], lat_courant[:, -1]], axis=0), "lat", northward
    )
    from_above = lax.ppermute(flat_fields[:, 0], "lat", southward)
    wide_fields = jnp.concatenate(
        [from_west[:stacked, :, None], flat_fields, from_east[:, :, None]], axis=2
    ).reshape(field_count, level_count, rows_dev, columns + 2)
    wide_courant = jnp.concatenate([from_west[stacked:, :, None], lon_courant], axis=2)
    column_flux = face_flux(wide_courant, wide_fields[..., :-1], wide_fields[..., 1:])
    tall_fields = jnp.concatenate(
        [from_below[:stacked, None], flat_fields, from_above[:, None]], axis=1
    ).reshape(field_count, level_count, rows_dev + 2, columns)
    tall_courant = jnp.concatenate([from_below[stacked:, None], lat_courant], axis=1)
    row_flux = face_flux(tall_courant, tall_fields[:, :, :-1], tall_fields[:, :, 1:])
    tile_index = lax.axis_index("lat")
    lower_row = tile_index * rows_dev - 1 + jnp.arange(rows_dev + 1, dtype=jnp.int32)
    row_flux = jnp.where((lower_row == rows_dev * lat_devices - 1)[:, None], 0.0, row_flux)
    increment = -(column_flux[..., 1:] - column_flux[..., :-1]) - (
        row_flux[:, :, 1:] - row_flux[:, :, :-1]
    )
    flat_increment = increment.reshape(stacked, rows_dev, columns)
    half_rows = rows_dev // 2
    pair_shift = lat_devices // 2
    pair_perm = [(i, (i + pair_shift) % lat_devices) for i in range(lat_devices)]
    is_low = tile_index < pair_shift
    partner_index = (tile_index + pair_shift) % lat_devices

    def row_info(tile):
        row_global = tile * rows_dev + jnp.arange(rows_dev, dtype=jnp.int32)
        matched = filter_rows[None, :] == row_global[:, None]
        return jnp.any(matched, axis=1), jnp.sum(jnp.where(matched, cutoff[None, :], 0), axis=1)

    is_filtered, own_cut = row_info(tile_index)
    _, partner_cut = row_info(partner_index)
    row_cut = jnp.where(is_filtered, own_cut, partner_cut).astype(jnp.float32)
    low_half = flat_increment[:, :half_rows]
    high_half = flat_increment[:, half_rows:]
    kept = jnp.where(is_low, low_half, high_half)
    given = jnp.where(is_low, high_half, low_half)
    kept_filtered = jnp.where(is_low, is_filtered[:half_rows], is_filtered[half_rows:])
    kept_cut = jnp.where(is_low, row_cut[:half_rows], row_cut[half_rows:])
    chunk_sizes = (stacked * 4 // 5, stacked - stacked * 4 // 5)
    returned_parts, handed_parts = [], []
    chunk_start = 0
    for chunk_stack in chunk_sizes:
        rows_of_part = slice(chunk_start, chunk_start + chunk_stack)
        chunk_start += chunk_stack
        line_count = chunk_stack * half_rows // lon_devices
        line_index = lax.axis_index("lon") * line_count + jnp.arange(line_count, dtype=jnp.int32)
        line_cut = kept_cut[line_index % half_rows]
        taken = lax.ppermute(given[rows_of_part], "lat", pair_perm)
        pair_lines = jnp.where(kept_filtered[None, :, None], kept[rows_of_part], taken)
        full_lines = lax.all_to_all(
            pair_lines.reshape(chunk_stack * half_rows, columns),
            "lon",
            split_axis=0,
            concat_axis=1,
            tiled=True,
        )
        smoothed = filter_lines(full_lines, line_cut)
        returned = lax.all_to_all(
            smoothed, "lon", split_axis=1, concat_axis=0, tiled=True
        ).reshape(chunk_stack, half_rows, columns)
        returned_parts.append(returned)
        handed_parts.append(lax.ppermute(returned, "lat", pair_perm))
    returned = jnp.concatenate(returned_parts, axis=0)
    handed_back = jnp.concatenate(handed_parts, axis=0)
    smooth_rows = jnp.where(
        is_low,
        jnp.concatenate([returned, handed_back], axis=1),
        jnp.concatenate([handed_back, returned], axis=1),
    )
    final_increment = jnp.where(is_filtered[None, :, None], smooth_rows, flat_increment)
    return (flat_fields + final_increment).reshape(fields.shape)


def solution(mesh):
    placed = (P(None, None, "lat", "lon"), P(None, "lat", "lon"), P(None, "lat", "lon"), P(), P())
    return jax.shard_map(
        body, mesh=mesh, in_specs=placed, out_specs=P(None, None, "lat", "lon"), check_vma=False
    )
```

```python
from functools import partial
import math

import jax
import jax.numpy as jnp
from jax import lax
from jax.sharding import PartitionSpec as P

radix_len = 128


def phase_table(row_total, col_total, modulus):
    product = (
        jnp.arange(row_total, dtype=jnp.int32)[:, None]
        * jnp.arange(col_total, dtype=jnp.int32)[None, :]
        % modulus
    )
    angle = product.astype(jnp.float32) * (2.0 * math.pi / modulus)
    return (jnp.cos(angle), jnp.sin(angle))


def filter_lines(lines, line_cut, lines_im=None):
    line_total, circle = lines.shape
    outer = circle // radix_len
    mixer = partial(jnp.einsum, precision=lax.Precision.HIGH)
    outer_cos, outer_sin = phase_table(outer, outer, outer)
    inner_cos, inner_sin = phase_table(radix_len, radix_len, radix_len)
    twist_cos, twist_sin = phase_table(outer, radix_len, circle)
    values = lines.reshape(line_total, outer, radix_len)
    first_re = mixer("lan,aj->ljn", values, outer_cos)
    first_im = -mixer("lan,aj->ljn", values, outer_sin)
    if lines_im is not None:
        values_im = lines_im.reshape(line_total, outer, radix_len)
        first_re = first_re + mixer("lan,aj->ljn", values_im, outer_sin)
        first_im = first_im + mixer("lan,aj->ljn", values_im, outer_cos)
    turned_re = first_re * twist_cos + first_im * twist_sin
    turned_im = first_im * twist_cos - first_re * twist_sin
    spec_re = mixer("ljn,nk->ljk", turned_re, inner_cos) + mixer(
        "ljn,nk->ljk", turned_im, inner_sin
    )
    spec_im = mixer("ljn,nk->ljk", turned_im, inner_cos) - mixer(
        "ljn,nk->ljk", turned_re, inner_sin
    )
    wave = (
        jnp.arange(outer, dtype=jnp.int32)[:, None]
        + outer * jnp.arange(radix_len, dtype=jnp.int32)[None, :]
    )
    mode_value = jnp.minimum(wave, circle - wave).astype(jnp.float32)[None]
    cut_value = line_cut[:, None, None]
    damp = jnp.where(mode_value <= cut_value, 1.0, (cut_value / jnp.maximum(mode_value, 1.0)) ** 2)
    spec_re = spec_re * damp
    spec_im = spec_im * damp
    back_re = mixer("ljk,kn->ljn", spec_re, inner_cos) - mixer("ljk,kn->ljn", spec_im, inner_sin)
    back_im = mixer("ljk,kn->ljn", spec_im, inner_cos) + mixer("ljk,kn->ljn", spec_re, inner_sin)
    untwist_re = back_re * twist_cos - back_im * twist_sin
    untwist_im = back_im * twist_cos + back_re * twist_sin
    result = mixer("ljn,ja->lan", untwist_re, outer_cos) - mixer(
        "ljn,ja->lan", untwist_im, outer_sin
    )
    if lines_im is None:
        return (result / circle).reshape(line_total, circle)
    result_im = mixer("ljn,ja->lan", untwist_im, outer_cos) + mixer(
        "ljn,ja->lan", untwist_re, outer_sin
    )
    return (
        (result / circle).reshape(line_total, circle),
        (result_im / circle).reshape(line_total, circle),
    )


def face_flux(courant, near_value, far_value):
    return 0.5 * courant * (near_value + far_value) - 0.5 * courant * courant * (
        far_value - near_value
    )


def body(fields, lon_courant, lat_courant, filter_rows, cutoff):
    field_count, level_count, rows_dev, columns = fields.shape
    stacked = field_count * level_count
    lon_devices = lax.axis_size("lon")
    lat_devices = lax.axis_size("lat")
    flat_fields = fields.reshape(stacked, rows_dev, columns)
    eastward = [(i, (i + 1) % lon_devices) for i in range(lon_devices)]
    westward = [((i + 1) % lon_devices, i) for i in range(lon_devices)]
    northward = [(i, i + 1) for i in range(lat_devices - 1)]
    southward = [(i + 1, i) for i in range(lat_devices - 1)]
    from_west = lax.ppermute(
        jnp.concatenate([flat_fields[..., -1], lon_courant[..., -1]], axis=0), "lon", eastward
    )
    from_east = lax.ppermute(flat_fields[..., 0], "lon", westward)
    from_below = lax.ppermute(
        jnp.concatenate([flat_fields[:, -1], lat_courant[:, -1]], axis=0), "lat", northward
    )
    from_above = lax.ppermute(flat_fields[:, 0], "lat", southward)
    wide_fields = jnp.concatenate(
        [from_west[:stacked, :, None], flat_fields, from_east[:, :, None]], axis=2
    ).reshape(field_count, level_count, rows_dev, columns + 2)
    wide_courant = jnp.concatenate([from_west[stacked:, :, None], lon_courant], axis=2)
    column_flux = face_flux(wide_courant, wide_fields[..., :-1], wide_fields[..., 1:])
    tall_fields = jnp.concatenate(
        [from_below[:stacked, None], flat_fields, from_above[:, None]], axis=1
    ).reshape(field_count, level_count, rows_dev + 2, columns)
    tall_courant = jnp.concatenate([from_below[stacked:, None], lat_courant], axis=1)
    row_flux = face_flux(tall_courant, tall_fields[:, :, :-1], tall_fields[:, :, 1:])
    tile_index = lax.axis_index("lat")
    lower_row = tile_index * rows_dev - 1 + jnp.arange(rows_dev + 1, dtype=jnp.int32)
    row_flux = jnp.where((lower_row == rows_dev * lat_devices - 1)[:, None], 0.0, row_flux)
    increment = -(column_flux[..., 1:] - column_flux[..., :-1]) - (
        row_flux[:, :, 1:] - row_flux[:, :, :-1]
    )
    flat_increment = increment.reshape(stacked, rows_dev, columns)
    half_rows = rows_dev // 2
    pair_shift = lat_devices // 2
    pair_perm = [(i, (i + pair_shift) % lat_devices) for i in range(lat_devices)]
    is_low = tile_index < pair_shift
    partner_index = (tile_index + pair_shift) % lat_devices

    def row_info(tile):
        row_global = tile * rows_dev + jnp.arange(rows_dev, dtype=jnp.int32)
        matched = filter_rows[None, :] == row_global[:, None]
        return jnp.any(matched, axis=1), jnp.sum(jnp.where(matched, cutoff[None, :], 0), axis=1)

    is_filtered, own_cut = row_info(tile_index)
    _, partner_cut = row_info(partner_index)
    row_cut = jnp.where(is_filtered, own_cut, partner_cut).astype(jnp.float32)
    low_half = flat_increment[:, :half_rows]
    high_half = flat_increment[:, half_rows:]
    kept = jnp.where(is_low, low_half, high_half)
    given = jnp.where(is_low, high_half, low_half)
    kept_filtered = jnp.where(is_low, is_filtered[:half_rows], is_filtered[half_rows:])
    kept_cut = jnp.where(is_low, row_cut[:half_rows], row_cut[half_rows:])
    chunk_sizes = (stacked * 3 // 5, stacked - stacked * 3 // 5)
    returned_parts, handed_parts = [], []
    chunk_start = 0
    for chunk_stack in chunk_sizes:
        rows_of_part = slice(chunk_start, chunk_start + chunk_stack)
        chunk_start += chunk_stack
        line_count = chunk_stack * half_rows // lon_devices
        line_index = lax.axis_index("lon") * line_count + jnp.arange(line_count, dtype=jnp.int32)
        line_cut = kept_cut[line_index % half_rows]
        taken = lax.ppermute(given[rows_of_part], "lat", pair_perm)
        pair_lines = jnp.where(kept_filtered[None, :, None], kept[rows_of_part], taken)
        full_lines = lax.all_to_all(
            pair_lines.reshape(chunk_stack * half_rows, columns),
            "lon",
            split_axis=0,
            concat_axis=1,
            tiled=True,
        )
        if line_count % (2 * half_rows) == 0:
            groups = line_count // (2 * half_rows)
            paired = full_lines.reshape(groups, 2, half_rows, full_lines.shape[1])
            pair_cut = line_cut.reshape(groups, 2, half_rows)[:, 0].reshape(-1)
            smooth_re, smooth_im = filter_lines(
                paired[:, 0].reshape(groups * half_rows, -1),
                pair_cut,
                paired[:, 1].reshape(groups * half_rows, -1),
            )
            smoothed = jnp.stack(
                [
                    smooth_re.reshape(groups, half_rows, -1),
                    smooth_im.reshape(groups, half_rows, -1),
                ],
                axis=1,
            ).reshape(full_lines.shape)
        else:
            smoothed = filter_lines(full_lines, line_cut)
        returned = lax.all_to_all(
            smoothed, "lon", split_axis=1, concat_axis=0, tiled=True
        ).reshape(chunk_stack, half_rows, columns)
        returned_parts.append(returned)
        handed_parts.append(lax.ppermute(returned, "lat", pair_perm))
    returned = jnp.concatenate(returned_parts, axis=0)
    handed_back = jnp.concatenate(handed_parts, axis=0)
    smooth_rows = jnp.where(
        is_low,
        jnp.concatenate([returned, handed_back], axis=1),
        jnp.concatenate([handed_back, returned], axis=1),
    )
    final_increment = jnp.where(is_filtered[None, :, None], smooth_rows, flat_increment)
    return (flat_fields + final_increment).reshape(fields.shape)


def solution(mesh):
    placed = (P(None, None, "lat", "lon"), P(None, "lat", "lon"), P(None, "lat", "lon"), P(), P())
    return jax.shard_map(
        body, mesh=mesh, in_specs=placed, out_specs=P(None, None, "lat", "lon"), check_vma=False
    )
```

```python
from functools import partial
import math

import jax
import jax.numpy as jnp
from jax import lax
from jax.sharding import PartitionSpec as P

radix_len = 128


def phase_table(row_total, col_total, modulus):
    product = (
        jnp.arange(row_total, dtype=jnp.int32)[:, None]
        * jnp.arange(col_total, dtype=jnp.int32)[None, :]
        % modulus
    )
    angle = product.astype(jnp.float32) * (2.0 * math.pi / modulus)
    return (jnp.cos(angle), jnp.sin(angle))


def filter_lines(lines, line_cut):
    line_total, circle = lines.shape
    outer = circle // radix_len
    mixer = partial(jnp.einsum, precision=lax.Precision.HIGH)
    outer_cos, outer_sin = phase_table(outer, outer, outer)
    inner_cos, inner_sin = phase_table(radix_len, radix_len, radix_len)
    twist_cos, twist_sin = phase_table(outer, radix_len, circle)
    values = lines.reshape(line_total, outer, radix_len)
    first_re = mixer("lan,aj->ljn", values, outer_cos)
    first_im = -mixer("lan,aj->ljn", values, outer_sin)
    turned_re = first_re * twist_cos + first_im * twist_sin
    turned_im = first_im * twist_cos - first_re * twist_sin
    spec_re = mixer("ljn,nk->ljk", turned_re, inner_cos) + mixer(
        "ljn,nk->ljk", turned_im, inner_sin
    )
    spec_im = mixer("ljn,nk->ljk", turned_im, inner_cos) - mixer(
        "ljn,nk->ljk", turned_re, inner_sin
    )
    wave = (
        jnp.arange(outer, dtype=jnp.int32)[:, None]
        + outer * jnp.arange(radix_len, dtype=jnp.int32)[None, :]
    )
    mode_value = jnp.minimum(wave, circle - wave).astype(jnp.float32)[None]
    cut_value = line_cut[:, None, None]
    damp = jnp.where(mode_value <= cut_value, 1.0, (cut_value / jnp.maximum(mode_value, 1.0)) ** 2)
    spec_re = spec_re * damp
    spec_im = spec_im * damp
    back_re = mixer("ljk,kn->ljn", spec_re, inner_cos) - mixer("ljk,kn->ljn", spec_im, inner_sin)
    back_im = mixer("ljk,kn->ljn", spec_im, inner_cos) + mixer("ljk,kn->ljn", spec_re, inner_sin)
    untwist_re = back_re * twist_cos - back_im * twist_sin
    untwist_im = back_im * twist_cos + back_re * twist_sin
    result = mixer("ljn,ja->lan", untwist_re, outer_cos) - mixer(
        "ljn,ja->lan", untwist_im, outer_sin
    )
    return (result / circle).reshape(line_total, circle)


def face_flux(courant, near_value, far_value):
    return 0.5 * courant * (near_value + far_value) - 0.5 * courant * courant * (
        far_value - near_value
    )


def body(fields, lon_courant, lat_courant, filter_rows, cutoff):
    field_count, level_count, rows_dev, columns = fields.shape
    stacked = field_count * level_count
    lon_devices = lax.axis_size("lon")
    lat_devices = lax.axis_size("lat")
    flat_fields = fields.reshape(stacked, rows_dev, columns)
    eastward = [(i, (i + 1) % lon_devices) for i in range(lon_devices)]
    westward = [((i + 1) % lon_devices, i) for i in range(lon_devices)]
    northward = [(i, i + 1) for i in range(lat_devices - 1)]
    southward = [(i + 1, i) for i in range(lat_devices - 1)]
    from_west = lax.ppermute(
        jnp.concatenate([flat_fields[..., -1], lon_courant[..., -1]], axis=0), "lon", eastward
    )
    from_east = lax.ppermute(flat_fields[..., 0], "lon", westward)
    from_below = lax.ppermute(
        jnp.concatenate([flat_fields[:, -1], lat_courant[:, -1]], axis=0), "lat", northward
    )
    from_above = lax.ppermute(flat_fields[:, 0], "lat", southward)
    wide_fields = jnp.concatenate(
        [from_west[:stacked, :, None], flat_fields, from_east[:, :, None]], axis=2
    ).reshape(field_count, level_count, rows_dev, columns + 2)
    wide_courant = jnp.concatenate([from_west[stacked:, :, None], lon_courant], axis=2)
    column_flux = face_flux(wide_courant, wide_fields[..., :-1], wide_fields[..., 1:])
    tall_fields = jnp.concatenate(
        [from_below[:stacked, None], flat_fields, from_above[:, None]], axis=1
    ).reshape(field_count, level_count, rows_dev + 2, columns)
    tall_courant = jnp.concatenate([from_below[stacked:, None], lat_courant], axis=1)
    row_flux = face_flux(tall_courant, tall_fields[:, :, :-1], tall_fields[:, :, 1:])
    tile_index = lax.axis_index("lat")
    lower_row = tile_index * rows_dev - 1 + jnp.arange(rows_dev + 1, dtype=jnp.int32)
    row_flux = jnp.where((lower_row == rows_dev * lat_devices - 1)[:, None], 0.0, row_flux)
    increment = -(column_flux[..., 1:] - column_flux[..., :-1]) - (
        row_flux[:, :, 1:] - row_flux[:, :, :-1]
    )
    flat_increment = increment.reshape(stacked, rows_dev, columns)
    half_rows = rows_dev // 2
    pair_shift = lat_devices // 2
    filter_count = filter_rows.shape[0]
    fewest_north, most_north = filter_count // 4, 3 * filter_count // 4
    low_gives = [a for a in range(pair_shift) if rows_dev * a + half_rows < most_north]
    high_gives = [a for a in range(pair_shift) if fewest_north <= rows_dev * a + half_rows - 1]
    forward_perm = [(a, a + pair_shift) for a in low_gives] + [
        (a + pair_shift, a) for a in high_gives
    ]
    backward_perm = [(a + pair_shift, a) for a in low_gives] + [
        (a, a + pair_shift) for a in high_gives
    ]
    is_low = tile_index < pair_shift
    partner_index = (tile_index + pair_shift) % lat_devices

    def row_info(tile):
        row_global = tile * rows_dev + jnp.arange(rows_dev, dtype=jnp.int32)
        matched = filter_rows[None, :] == row_global[:, None]
        return jnp.any(matched, axis=1), jnp.sum(jnp.where(matched, cutoff[None, :], 0), axis=1)

    is_filtered, own_cut = row_info(tile_index)
    _, partner_cut = row_info(partner_index)
    row_cut = jnp.where(is_filtered, own_cut, partner_cut).astype(jnp.float32)
    low_half = flat_increment[:, :half_rows]
    high_half = flat_increment[:, half_rows:]
    kept = jnp.where(is_low, low_half, high_half)
    given = jnp.where(is_low, high_half, low_half)
    kept_filtered = jnp.where(is_low, is_filtered[:half_rows], is_filtered[half_rows:])
    kept_cut = jnp.where(is_low, row_cut[:half_rows], row_cut[half_rows:])
    chunk_sizes = (stacked * 2 // 5, stacked - stacked * 2 // 5)
    returned_parts, handed_parts = [], []
    chunk_start = 0
    for chunk_stack in chunk_sizes:
        rows_of_part = slice(chunk_start, chunk_start + chunk_stack)
        chunk_start += chunk_stack
        line_count = chunk_stack * half_rows // lon_devices
        line_index = lax.axis_index("lon") * line_count + jnp.arange(line_count, dtype=jnp.int32)
        line_cut = kept_cut[line_index % half_rows]
        taken = lax.ppermute(given[rows_of_part], "lat", forward_perm)
        pair_lines = jnp.where(kept_filtered[None, :, None], kept[rows_of_part], taken)
        full_lines = lax.all_to_all(
            pair_lines.reshape(chunk_stack * half_rows, columns),
            "lon",
            split_axis=0,
            concat_axis=1,
            tiled=True,
        )
        smoothed = filter_lines(full_lines, line_cut)
        returned = lax.all_to_all(
            smoothed, "lon", split_axis=1, concat_axis=0, tiled=True
        ).reshape(chunk_stack, half_rows, columns)
        returned_parts.append(returned)
        handed_parts.append(lax.ppermute(returned, "lat", backward_perm))
    returned = jnp.concatenate(returned_parts, axis=0)
    handed_back = jnp.concatenate(handed_parts, axis=0)
    smooth_rows = jnp.where(
        is_low,
        jnp.concatenate([returned, handed_back], axis=1),
        jnp.concatenate([handed_back, returned], axis=1),
    )
    final_increment = jnp.where(is_filtered[None, :, None], smooth_rows, flat_increment)
    return (flat_fields + final_increment).reshape(fields.shape)


def solution(mesh):
    placed = (P(None, None, "lat", "lon"), P(None, "lat", "lon"), P(None, "lat", "lon"), P(), P())
    return jax.shard_map(
        body, mesh=mesh, in_specs=placed, out_specs=P(None, None, "lat", "lon"), check_vma=False
    )
```

```python
from functools import partial
import math

import jax
import jax.numpy as jnp
from jax import lax
from jax.sharding import PartitionSpec as P

radix_len = 128


def phase_table(row_total, col_total, modulus):
    product = (
        jnp.arange(row_total, dtype=jnp.int32)[:, None]
        * jnp.arange(col_total, dtype=jnp.int32)[None, :]
        % modulus
    )
    angle = product.astype(jnp.float32) * (2.0 * math.pi / modulus)
    return (jnp.cos(angle), jnp.sin(angle))


def filter_lines(lines, line_cut):
    circle = lines.shape[1]
    spectrum = jnp.fft.rfft(lines, axis=-1)
    mode_value = jnp.arange(circle // 2 + 1, dtype=jnp.float32)[None, :]
    cut_value = line_cut[:, None]
    damp = jnp.where(mode_value <= cut_value, 1.0, (cut_value / jnp.maximum(mode_value, 1.0)) ** 2)
    return jnp.fft.irfft(spectrum * damp, n=circle, axis=-1).astype(lines.dtype)


def face_flux(courant, near_value, far_value):
    return 0.5 * courant * (near_value + far_value) - 0.5 * courant * courant * (
        far_value - near_value
    )


def body(fields, lon_courant, lat_courant, filter_rows, cutoff):
    field_count, level_count, rows_dev, columns = fields.shape
    stacked = field_count * level_count
    lon_devices = lax.axis_size("lon")
    lat_devices = lax.axis_size("lat")
    flat_fields = fields.reshape(stacked, rows_dev, columns)
    eastward = [(i, (i + 1) % lon_devices) for i in range(lon_devices)]
    westward = [((i + 1) % lon_devices, i) for i in range(lon_devices)]
    northward = [(i, i + 1) for i in range(lat_devices - 1)]
    southward = [(i + 1, i) for i in range(lat_devices - 1)]
    from_west = lax.ppermute(
        jnp.concatenate([flat_fields[..., -1], lon_courant[..., -1]], axis=0), "lon", eastward
    )
    from_east = lax.ppermute(flat_fields[..., 0], "lon", westward)
    from_below = lax.ppermute(
        jnp.concatenate([flat_fields[:, -1], lat_courant[:, -1]], axis=0), "lat", northward
    )
    from_above = lax.ppermute(flat_fields[:, 0], "lat", southward)
    wide_fields = jnp.concatenate(
        [from_west[:stacked, :, None], flat_fields, from_east[:, :, None]], axis=2
    ).reshape(field_count, level_count, rows_dev, columns + 2)
    wide_courant = jnp.concatenate([from_west[stacked:, :, None], lon_courant], axis=2)
    column_flux = face_flux(wide_courant, wide_fields[..., :-1], wide_fields[..., 1:])
    tall_fields = jnp.concatenate(
        [from_below[:stacked, None], flat_fields, from_above[:, None]], axis=1
    ).reshape(field_count, level_count, rows_dev + 2, columns)
    tall_courant = jnp.concatenate([from_below[stacked:, None], lat_courant], axis=1)
    row_flux = face_flux(tall_courant, tall_fields[:, :, :-1], tall_fields[:, :, 1:])
    tile_index = lax.axis_index("lat")
    lower_row = tile_index * rows_dev - 1 + jnp.arange(rows_dev + 1, dtype=jnp.int32)
    row_flux = jnp.where((lower_row == rows_dev * lat_devices - 1)[:, None], 0.0, row_flux)
    increment = -(column_flux[..., 1:] - column_flux[..., :-1]) - (
        row_flux[:, :, 1:] - row_flux[:, :, :-1]
    )
    flat_increment = increment.reshape(stacked, rows_dev, columns)
    half_rows = rows_dev // 2
    pair_shift = lat_devices // 2
    pair_perm = [(i, (i + pair_shift) % lat_devices) for i in range(lat_devices)]
    is_low = tile_index < pair_shift
    partner_index = (tile_index + pair_shift) % lat_devices

    def row_info(tile):
        row_global = tile * rows_dev + jnp.arange(rows_dev, dtype=jnp.int32)
        matched = filter_rows[None, :] == row_global[:, None]
        return jnp.any(matched, axis=1), jnp.sum(jnp.where(matched, cutoff[None, :], 0), axis=1)

    is_filtered, own_cut = row_info(tile_index)
    _, partner_cut = row_info(partner_index)
    row_cut = jnp.where(is_filtered, own_cut, partner_cut).astype(jnp.float32)
    low_half = flat_increment[:, :half_rows]
    high_half = flat_increment[:, half_rows:]
    kept = jnp.where(is_low, low_half, high_half)
    given = jnp.where(is_low, high_half, low_half)
    kept_filtered = jnp.where(is_low, is_filtered[:half_rows], is_filtered[half_rows:])
    kept_cut = jnp.where(is_low, row_cut[:half_rows], row_cut[half_rows:])
    chunk_sizes = (stacked * 2 // 5, stacked - stacked * 2 // 5)
    returned_parts, handed_parts = [], []
    chunk_start = 0
    for chunk_stack in chunk_sizes:
        rows_of_part = slice(chunk_start, chunk_start + chunk_stack)
        chunk_start += chunk_stack
        line_count = chunk_stack * half_rows // lon_devices
        line_index = lax.axis_index("lon") * line_count + jnp.arange(line_count, dtype=jnp.int32)
        line_cut = kept_cut[line_index % half_rows]
        taken = lax.ppermute(given[rows_of_part], "lat", pair_perm)
        pair_lines = jnp.where(kept_filtered[None, :, None], kept[rows_of_part], taken)
        full_lines = lax.all_to_all(
            pair_lines.reshape(chunk_stack * half_rows, columns),
            "lon",
            split_axis=0,
            concat_axis=1,
            tiled=True,
        )
        smoothed = filter_lines(full_lines, line_cut)
        returned = lax.all_to_all(
            smoothed, "lon", split_axis=1, concat_axis=0, tiled=True
        ).reshape(chunk_stack, half_rows, columns)
        returned_parts.append(returned)
        handed_parts.append(lax.ppermute(returned, "lat", pair_perm))
    returned = jnp.concatenate(returned_parts, axis=0)
    handed_back = jnp.concatenate(handed_parts, axis=0)
    smooth_rows = jnp.where(
        is_low,
        jnp.concatenate([returned, handed_back], axis=1),
        jnp.concatenate([handed_back, returned], axis=1),
    )
    final_increment = jnp.where(is_filtered[None, :, None], smooth_rows, flat_increment)
    return (flat_fields + final_increment).reshape(fields.shape)


def solution(mesh):
    placed = (P(None, None, "lat", "lon"), P(None, "lat", "lon"), P(None, "lat", "lon"), P(), P())
    return jax.shard_map(
        body, mesh=mesh, in_specs=placed, out_specs=P(None, None, "lat", "lon"), check_vma=False
    )
```

```python
from functools import partial
import math

import jax
import jax.numpy as jnp
from jax import lax
from jax.sharding import PartitionSpec as P

radix_len = 384


def phase_table(row_total, col_total, modulus):
    product = (
        jnp.arange(row_total, dtype=jnp.int32)[:, None]
        * jnp.arange(col_total, dtype=jnp.int32)[None, :]
        % modulus
    )
    angle = product.astype(jnp.float32) * (2.0 * math.pi / modulus)
    return (jnp.cos(angle), jnp.sin(angle))


def filter_lines(lines, line_cut):
    line_total, circle = lines.shape
    outer = circle // radix_len
    mixer = partial(jnp.einsum, precision=lax.Precision.HIGH)
    outer_cos, outer_sin = phase_table(outer, outer, outer)
    inner_cos, inner_sin = phase_table(radix_len, radix_len, radix_len)
    twist_cos, twist_sin = phase_table(outer, radix_len, circle)
    values = lines.reshape(line_total, outer, radix_len)
    first_re = mixer("lan,aj->ljn", values, outer_cos)
    first_im = -mixer("lan,aj->ljn", values, outer_sin)
    turned_re = first_re * twist_cos + first_im * twist_sin
    turned_im = first_im * twist_cos - first_re * twist_sin
    spec_re = mixer("ljn,nk->ljk", turned_re, inner_cos) + mixer(
        "ljn,nk->ljk", turned_im, inner_sin
    )
    spec_im = mixer("ljn,nk->ljk", turned_im, inner_cos) - mixer(
        "ljn,nk->ljk", turned_re, inner_sin
    )
    wave = (
        jnp.arange(outer, dtype=jnp.int32)[:, None]
        + outer * jnp.arange(radix_len, dtype=jnp.int32)[None, :]
    )
    mode_value = jnp.minimum(wave, circle - wave).astype(jnp.float32)[None]
    cut_value = line_cut[:, None, None]
    damp = jnp.where(mode_value <= cut_value, 1.0, (cut_value / jnp.maximum(mode_value, 1.0)) ** 2)
    spec_re = spec_re * damp
    spec_im = spec_im * damp
    back_re = mixer("ljk,kn->ljn", spec_re, inner_cos) - mixer("ljk,kn->ljn", spec_im, inner_sin)
    back_im = mixer("ljk,kn->ljn", spec_im, inner_cos) + mixer("ljk,kn->ljn", spec_re, inner_sin)
    untwist_re = back_re * twist_cos - back_im * twist_sin
    untwist_im = back_im * twist_cos + back_re * twist_sin
    result = mixer("ljn,ja->lan", untwist_re, outer_cos) - mixer(
        "ljn,ja->lan", untwist_im, outer_sin
    )
    return (result / circle).reshape(line_total, circle)


def face_flux(courant, near_value, far_value):
    return 0.5 * courant * (near_value + far_value) - 0.5 * courant * courant * (
        far_value - near_value
    )


def body(fields, lon_courant, lat_courant, filter_rows, cutoff):
    field_count, level_count, rows_dev, columns = fields.shape
    stacked = field_count * level_count
    lon_devices = lax.axis_size("lon")
    lat_devices = lax.axis_size("lat")
    flat_fields = fields.reshape(stacked, rows_dev, columns)
    eastward = [(i, (i + 1) % lon_devices) for i in range(lon_devices)]
    westward = [((i + 1) % lon_devices, i) for i in range(lon_devices)]
    northward = [(i, i + 1) for i in range(lat_devices - 1)]
    southward = [(i + 1, i) for i in range(lat_devices - 1)]
    from_west = lax.ppermute(
        jnp.concatenate([flat_fields[..., -1], lon_courant[..., -1]], axis=0), "lon", eastward
    )
    from_east = lax.ppermute(flat_fields[..., 0], "lon", westward)
    from_below = lax.ppermute(
        jnp.concatenate([flat_fields[:, -1], lat_courant[:, -1]], axis=0), "lat", northward
    )
    from_above = lax.ppermute(flat_fields[:, 0], "lat", southward)
    wide_fields = jnp.concatenate(
        [from_west[:stacked, :, None], flat_fields, from_east[:, :, None]], axis=2
    ).reshape(field_count, level_count, rows_dev, columns + 2)
    wide_courant = jnp.concatenate([from_west[stacked:, :, None], lon_courant], axis=2)
    column_flux = face_flux(wide_courant, wide_fields[..., :-1], wide_fields[..., 1:])
    tall_fields = jnp.concatenate(
        [from_below[:stacked, None], flat_fields, from_above[:, None]], axis=1
    ).reshape(field_count, level_count, rows_dev + 2, columns)
    tall_courant = jnp.concatenate([from_below[stacked:, None], lat_courant], axis=1)
    row_flux = face_flux(tall_courant, tall_fields[:, :, :-1], tall_fields[:, :, 1:])
    tile_index = lax.axis_index("lat")
    lower_row = tile_index * rows_dev - 1 + jnp.arange(rows_dev + 1, dtype=jnp.int32)
    row_flux = jnp.where((lower_row == rows_dev * lat_devices - 1)[:, None], 0.0, row_flux)
    increment = -(column_flux[..., 1:] - column_flux[..., :-1]) - (
        row_flux[:, :, 1:] - row_flux[:, :, :-1]
    )
    flat_increment = increment.reshape(stacked, rows_dev, columns)
    half_rows = rows_dev // 2
    pair_shift = lat_devices // 2
    pair_perm = [(i, (i + pair_shift) % lat_devices) for i in range(lat_devices)]
    is_low = tile_index < pair_shift
    partner_index = (tile_index + pair_shift) % lat_devices

    def row_info(tile):
        row_global = tile * rows_dev + jnp.arange(rows_dev, dtype=jnp.int32)
        matched = filter_rows[None, :] == row_global[:, None]
        return jnp.any(matched, axis=1), jnp.sum(jnp.where(matched, cutoff[None, :], 0), axis=1)

    is_filtered, own_cut = row_info(tile_index)
    _, partner_cut = row_info(partner_index)
    row_cut = jnp.where(is_filtered, own_cut, partner_cut).astype(jnp.float32)
    low_half = flat_increment[:, :half_rows]
    high_half = flat_increment[:, half_rows:]
    kept = jnp.where(is_low, low_half, high_half)
    given = jnp.where(is_low, high_half, low_half)
    kept_filtered = jnp.where(is_low, is_filtered[:half_rows], is_filtered[half_rows:])
    kept_cut = jnp.where(is_low, row_cut[:half_rows], row_cut[half_rows:])
    chunk_sizes = (stacked * 2 // 5, stacked - stacked * 2 // 5)
    returned_parts, handed_parts = [], []
    chunk_start = 0
    for chunk_stack in chunk_sizes:
        rows_of_part = slice(chunk_start, chunk_start + chunk_stack)
        chunk_start += chunk_stack
        line_count = chunk_stack * half_rows // lon_devices
        line_index = lax.axis_index("lon") * line_count + jnp.arange(line_count, dtype=jnp.int32)
        line_cut = kept_cut[line_index % half_rows]
        taken = lax.ppermute(given[rows_of_part], "lat", pair_perm)
        pair_lines = jnp.where(kept_filtered[None, :, None], kept[rows_of_part], taken)
        full_lines = lax.all_to_all(
            pair_lines.reshape(chunk_stack * half_rows, columns),
            "lon",
            split_axis=0,
            concat_axis=1,
            tiled=True,
        )
        smoothed = filter_lines(full_lines, line_cut)
        returned = lax.all_to_all(
            smoothed, "lon", split_axis=1, concat_axis=0, tiled=True
        ).reshape(chunk_stack, half_rows, columns)
        returned_parts.append(returned)
        handed_parts.append(lax.ppermute(returned, "lat", pair_perm))
    returned = jnp.concatenate(returned_parts, axis=0)
    handed_back = jnp.concatenate(handed_parts, axis=0)
    smooth_rows = jnp.where(
        is_low,
        jnp.concatenate([returned, handed_back], axis=1),
        jnp.concatenate([handed_back, returned], axis=1),
    )
    final_increment = jnp.where(is_filtered[None, :, None], smooth_rows, flat_increment)
    return (flat_fields + final_increment).reshape(fields.shape)


def solution(mesh):
    placed = (P(None, None, "lat", "lon"), P(None, "lat", "lon"), P(None, "lat", "lon"), P(), P())
    return jax.shard_map(
        body, mesh=mesh, in_specs=placed, out_specs=P(None, None, "lat", "lon"), check_vma=False
    )
```

```python
from functools import partial
import math

import jax
import jax.numpy as jnp
from jax import lax
from jax.sharding import PartitionSpec as P

radix_len = 128


def phase_table(row_total, col_total, modulus):
    product = (
        jnp.arange(row_total, dtype=jnp.int32)[:, None]
        * jnp.arange(col_total, dtype=jnp.int32)[None, :]
        % modulus
    )
    angle = product.astype(jnp.float32) * (2.0 * math.pi / modulus)
    return (jnp.cos(angle), jnp.sin(angle))


def filter_lines(lines, line_cut):
    line_total, circle = lines.shape
    outer = circle // radix_len
    mixer = partial(jnp.einsum, precision=lax.Precision.HIGH)
    outer_cos, outer_sin = phase_table(outer, outer, outer)
    inner_cos, inner_sin = phase_table(radix_len, radix_len, radix_len)
    twist_cos, twist_sin = phase_table(outer, radix_len, circle)
    values = lines.reshape(line_total, outer, radix_len)
    first_re = mixer("lan,aj->ljn", values, outer_cos)
    first_im = -mixer("lan,aj->ljn", values, outer_sin)
    turned_re = first_re * twist_cos + first_im * twist_sin
    turned_im = first_im * twist_cos - first_re * twist_sin
    spec_re = mixer("ljn,nk->ljk", turned_re, inner_cos) + mixer(
        "ljn,nk->ljk", turned_im, inner_sin
    )
    spec_im = mixer("ljn,nk->ljk", turned_im, inner_cos) - mixer(
        "ljn,nk->ljk", turned_re, inner_sin
    )
    wave = (
        jnp.arange(outer, dtype=jnp.int32)[:, None]
        + outer * jnp.arange(radix_len, dtype=jnp.int32)[None, :]
    )
    mode_value = jnp.minimum(wave, circle - wave).astype(jnp.float32)[None]
    cut_value = line_cut[:, None, None]
    damp = jnp.where(mode_value <= cut_value, 1.0, (cut_value / jnp.maximum(mode_value, 1.0)) ** 2)
    spec_re = spec_re * damp
    spec_im = spec_im * damp
    back_re = mixer("ljk,kn->ljn", spec_re, inner_cos) - mixer("ljk,kn->ljn", spec_im, inner_sin)
    back_im = mixer("ljk,kn->ljn", spec_im, inner_cos) + mixer("ljk,kn->ljn", spec_re, inner_sin)
    untwist_re = back_re * twist_cos - back_im * twist_sin
    untwist_im = back_im * twist_cos + back_re * twist_sin
    result = mixer("ljn,ja->lan", untwist_re, outer_cos) - mixer(
        "ljn,ja->lan", untwist_im, outer_sin
    )
    return (result / circle).reshape(line_total, circle)


def face_flux(courant, near_value, far_value):
    return 0.5 * courant * (near_value + far_value) - 0.5 * courant * courant * (
        far_value - near_value
    )


def body(fields, lon_courant, lat_courant, filter_rows, cutoff):
    field_count, level_count, rows_dev, columns = fields.shape
    stacked = field_count * level_count
    lon_devices = lax.axis_size("lon")
    lat_devices = lax.axis_size("lat")
    flat_fields = fields.reshape(stacked, rows_dev, columns)
    eastward = [(i, (i + 1) % lon_devices) for i in range(lon_devices)]
    westward = [((i + 1) % lon_devices, i) for i in range(lon_devices)]
    northward = [(i, i + 1) for i in range(lat_devices - 1)]
    southward = [(i + 1, i) for i in range(lat_devices - 1)]
    from_west = lax.ppermute(
        jnp.concatenate([flat_fields[..., -1], lon_courant[..., -1]], axis=0), "lon", eastward
    )
    from_east = lax.ppermute(flat_fields[..., 0], "lon", westward)
    from_below = lax.ppermute(
        jnp.concatenate([flat_fields[:, -1], lat_courant[:, -1]], axis=0), "lat", northward
    )
    from_above = lax.ppermute(flat_fields[:, 0], "lat", southward)
    wide_fields = jnp.concatenate(
        [from_west[:stacked, :, None], flat_fields, from_east[:, :, None]], axis=2
    ).reshape(field_count, level_count, rows_dev, columns + 2)
    wide_courant = jnp.concatenate([from_west[stacked:, :, None], lon_courant], axis=2)
    column_flux = face_flux(wide_courant, wide_fields[..., :-1], wide_fields[..., 1:])
    tall_fields = jnp.concatenate(
        [from_below[:stacked, None], flat_fields, from_above[:, None]], axis=1
    ).reshape(field_count, level_count, rows_dev + 2, columns)
    tall_courant = jnp.concatenate([from_below[stacked:, None], lat_courant], axis=1)
    row_flux = face_flux(tall_courant, tall_fields[:, :, :-1], tall_fields[:, :, 1:])
    tile_index = lax.axis_index("lat")
    lower_row = tile_index * rows_dev - 1 + jnp.arange(rows_dev + 1, dtype=jnp.int32)
    row_flux = jnp.where((lower_row == rows_dev * lat_devices - 1)[:, None], 0.0, row_flux)
    increment = -(column_flux[..., 1:] - column_flux[..., :-1]) - (
        row_flux[:, :, 1:] - row_flux[:, :, :-1]
    )
    flat_increment = increment.reshape(stacked, rows_dev, columns)
    half_rows = rows_dev // 2
    pair_shift = lat_devices // 2
    pair_perm = [(i, (i + pair_shift) % lat_devices) for i in range(lat_devices)]
    is_low = tile_index < pair_shift
    partner_index = (tile_index + pair_shift) % lat_devices

    def row_info(tile):
        row_global = tile * rows_dev + jnp.arange(rows_dev, dtype=jnp.int32)
        matched = filter_rows[None, :] == row_global[:, None]
        return jnp.any(matched, axis=1), jnp.sum(jnp.where(matched, cutoff[None, :], 0), axis=1)

    is_filtered, own_cut = row_info(tile_index)
    _, partner_cut = row_info(partner_index)
    row_cut = jnp.where(is_filtered, own_cut, partner_cut).astype(jnp.float32)
    low_half = flat_increment[:, :half_rows]
    high_half = flat_increment[:, half_rows:]
    kept_start = jnp.where(is_low, 0, half_rows)
    kept = lax.dynamic_slice_in_dim(flat_increment, kept_start, half_rows, axis=1)
    given = lax.dynamic_slice_in_dim(flat_increment, half_rows - kept_start, half_rows, axis=1)
    kept_filtered = jnp.where(is_low, is_filtered[:half_rows], is_filtered[half_rows:])
    kept_cut = jnp.where(is_low, row_cut[:half_rows], row_cut[half_rows:])
    chunk_sizes = (stacked * 2 // 5, stacked - stacked * 2 // 5)
    returned_parts, handed_parts = [], []
    chunk_start = 0
    for chunk_stack in chunk_sizes:
        rows_of_part = slice(chunk_start, chunk_start + chunk_stack)
        chunk_start += chunk_stack
        line_count = chunk_stack * half_rows // lon_devices
        line_index = lax.axis_index("lon") * line_count + jnp.arange(line_count, dtype=jnp.int32)
        line_cut = kept_cut[line_index % half_rows]
        taken = lax.ppermute(given[rows_of_part], "lat", pair_perm)
        pair_lines = jnp.where(kept_filtered[None, :, None], kept[rows_of_part], taken)
        full_lines = lax.all_to_all(
            pair_lines.reshape(chunk_stack * half_rows, columns),
            "lon",
            split_axis=0,
            concat_axis=1,
            tiled=True,
        )
        smoothed = filter_lines(full_lines, line_cut)
        returned = lax.all_to_all(
            smoothed, "lon", split_axis=1, concat_axis=0, tiled=True
        ).reshape(chunk_stack, half_rows, columns)
        returned_parts.append(returned)
        handed_parts.append(lax.ppermute(returned, "lat", pair_perm))
    returned = jnp.concatenate(returned_parts, axis=0)
    handed_back = jnp.concatenate(handed_parts, axis=0)
    smooth_rows = jnp.where(
        is_low,
        jnp.concatenate([returned, handed_back], axis=1),
        jnp.concatenate([handed_back, returned], axis=1),
    )
    final_increment = jnp.where(is_filtered[None, :, None], smooth_rows, flat_increment)
    return (flat_fields + final_increment).reshape(fields.shape)


def solution(mesh):
    placed = (P(None, None, "lat", "lon"), P(None, "lat", "lon"), P(None, "lat", "lon"), P(), P())
    return jax.shard_map(
        body, mesh=mesh, in_specs=placed, out_specs=P(None, None, "lat", "lon"), check_vma=False
    )
```

```python
from functools import partial
import math

import jax
import jax.numpy as jnp
from jax import lax
from jax.sharding import PartitionSpec as P

radix_len = 128


def phase_table(row_total, col_total, modulus):
    product = (
        jnp.arange(row_total, dtype=jnp.int32)[:, None]
        * jnp.arange(col_total, dtype=jnp.int32)[None, :]
        % modulus
    )
    angle = product.astype(jnp.float32) * (2.0 * math.pi / modulus)
    return (jnp.cos(angle), jnp.sin(angle))


def filter_lines(lines, line_cut):
    line_total, circle = lines.shape
    outer = circle // radix_len
    mixer = partial(jnp.einsum, precision=lax.Precision.HIGH)
    outer_cos, outer_sin = phase_table(outer, outer, outer)
    inner_cos, inner_sin = phase_table(radix_len, radix_len, radix_len)
    twist_cos, twist_sin = phase_table(outer, radix_len, circle)
    values = lines.reshape(line_total, outer, radix_len)
    first_re = mixer("lan,aj->ljn", values, outer_cos)
    first_im = -mixer("lan,aj->ljn", values, outer_sin)
    turned_re = first_re * twist_cos + first_im * twist_sin
    turned_im = first_im * twist_cos - first_re * twist_sin
    spec_re = mixer("ljn,nk->ljk", turned_re, inner_cos) + mixer(
        "ljn,nk->ljk", turned_im, inner_sin
    )
    spec_im = mixer("ljn,nk->ljk", turned_im, inner_cos) - mixer(
        "ljn,nk->ljk", turned_re, inner_sin
    )
    wave = (
        jnp.arange(outer, dtype=jnp.int32)[:, None]
        + outer * jnp.arange(radix_len, dtype=jnp.int32)[None, :]
    )
    mode_value = jnp.minimum(wave, circle - wave).astype(jnp.float32)[None]
    cut_value = line_cut[:, None, None]
    damp = jnp.where(mode_value <= cut_value, 1.0, (cut_value / jnp.maximum(mode_value, 1.0)) ** 2)
    spec_re = spec_re * damp
    spec_im = spec_im * damp
    back_re = mixer("ljk,kn->ljn", spec_re, inner_cos) - mixer("ljk,kn->ljn", spec_im, inner_sin)
    back_im = mixer("ljk,kn->ljn", spec_im, inner_cos) + mixer("ljk,kn->ljn", spec_re, inner_sin)
    untwist_re = back_re * twist_cos - back_im * twist_sin
    untwist_im = back_im * twist_cos + back_re * twist_sin
    result = mixer("ljn,ja->lan", untwist_re, outer_cos) - mixer(
        "ljn,ja->lan", untwist_im, outer_sin
    )
    return (result / circle).reshape(line_total, circle)


def face_flux(courant, near_value, far_value):
    return 0.5 * courant * (near_value + far_value) - 0.5 * courant * courant * (
        far_value - near_value
    )


def body(fields, lon_courant, lat_courant, filter_rows, cutoff):
    field_count, level_count, rows_dev, columns = fields.shape
    stacked = field_count * level_count
    lon_devices = lax.axis_size("lon")
    lat_devices = lax.axis_size("lat")
    flat_fields = fields.reshape(stacked, rows_dev, columns)
    eastward = [(i, (i + 1) % lon_devices) for i in range(lon_devices)]
    westward = [((i + 1) % lon_devices, i) for i in range(lon_devices)]
    northward = [(i, i + 1) for i in range(lat_devices - 1)]
    southward = [(i + 1, i) for i in range(lat_devices - 1)]
    from_west = lax.ppermute(
        jnp.concatenate([flat_fields[..., -1], lon_courant[..., -1]], axis=0), "lon", eastward
    )
    from_east = lax.ppermute(flat_fields[..., 0], "lon", westward)
    from_below = lax.ppermute(
        jnp.concatenate([flat_fields[:, -1], lat_courant[:, -1]], axis=0), "lat", northward
    )
    from_above = lax.ppermute(flat_fields[:, 0], "lat", southward)
    wide_fields = jnp.concatenate(
        [from_west[:stacked, :, None], flat_fields, from_east[:, :, None]], axis=2
    ).reshape(field_count, level_count, rows_dev, columns + 2)
    wide_courant = jnp.concatenate([from_west[stacked:, :, None], lon_courant], axis=2)
    column_flux = face_flux(wide_courant, wide_fields[..., :-1], wide_fields[..., 1:])
    tall_fields = jnp.concatenate(
        [from_below[:stacked, None], flat_fields, from_above[:, None]], axis=1
    ).reshape(field_count, level_count, rows_dev + 2, columns)
    tall_courant = jnp.concatenate([from_below[stacked:, None], lat_courant], axis=1)
    row_flux = face_flux(tall_courant, tall_fields[:, :, :-1], tall_fields[:, :, 1:])
    tile_index = lax.axis_index("lat")
    lower_row = tile_index * rows_dev - 1 + jnp.arange(rows_dev + 1, dtype=jnp.int32)
    row_flux = jnp.where((lower_row == rows_dev * lat_devices - 1)[:, None], 0.0, row_flux)
    increment = -(column_flux[..., 1:] - column_flux[..., :-1]) - (
        row_flux[:, :, 1:] - row_flux[:, :, :-1]
    )
    flat_increment = increment.reshape(stacked, rows_dev, columns)
    half_rows = rows_dev // 2
    pair_shift = lat_devices // 2
    pair_perm = [(i, (i + pair_shift) % lat_devices) for i in range(lat_devices)]
    is_low = tile_index < pair_shift
    partner_index = (tile_index + pair_shift) % lat_devices

    def row_info(tile):
        row_global = tile * rows_dev + jnp.arange(rows_dev, dtype=jnp.int32)
        matched = filter_rows[None, :] == row_global[:, None]
        return jnp.any(matched, axis=1), jnp.sum(jnp.where(matched, cutoff[None, :], 0), axis=1)

    is_filtered, own_cut = row_info(tile_index)
    _, partner_cut = row_info(partner_index)
    row_cut = jnp.where(is_filtered, own_cut, partner_cut).astype(jnp.float32)
    low_half = flat_increment[:, :half_rows]
    high_half = flat_increment[:, half_rows:]
    kept = jnp.where(is_low, low_half, high_half)
    given = jnp.where(is_low, high_half, low_half)
    kept_filtered = jnp.where(is_low, is_filtered[:half_rows], is_filtered[half_rows:])
    kept_cut = jnp.where(is_low, row_cut[:half_rows], row_cut[half_rows:])
    chunk_sizes = (stacked * 3 // 10, stacked - stacked * 3 // 10)
    returned_parts, handed_parts = [], []
    chunk_start = 0
    for chunk_stack in chunk_sizes:
        rows_of_part = slice(chunk_start, chunk_start + chunk_stack)
        chunk_start += chunk_stack
        line_count = chunk_stack * half_rows // lon_devices
        line_index = lax.axis_index("lon") * line_count + jnp.arange(line_count, dtype=jnp.int32)
        line_cut = kept_cut[line_index % half_rows]
        taken = lax.ppermute(given[rows_of_part], "lat", pair_perm)
        pair_lines = jnp.where(kept_filtered[None, :, None], kept[rows_of_part], taken)
        full_lines = lax.all_to_all(
            pair_lines.reshape(chunk_stack * half_rows, columns),
            "lon",
            split_axis=0,
            concat_axis=1,
            tiled=True,
        )
        smoothed = filter_lines(full_lines, line_cut)
        returned = lax.all_to_all(
            smoothed, "lon", split_axis=1, concat_axis=0, tiled=True
        ).reshape(chunk_stack, half_rows, columns)
        returned_parts.append(returned)
        handed_parts.append(lax.ppermute(returned, "lat", pair_perm))
    returned = jnp.concatenate(returned_parts, axis=0)
    handed_back = jnp.concatenate(handed_parts, axis=0)
    smooth_rows = jnp.where(
        is_low,
        jnp.concatenate([returned, handed_back], axis=1),
        jnp.concatenate([handed_back, returned], axis=1),
    )
    final_increment = jnp.where(is_filtered[None, :, None], smooth_rows, flat_increment)
    return (flat_fields + final_increment).reshape(fields.shape)


def solution(mesh):
    placed = (P(None, None, "lat", "lon"), P(None, "lat", "lon"), P(None, "lat", "lon"), P(), P())
    return jax.shard_map(
        body, mesh=mesh, in_specs=placed, out_specs=P(None, None, "lat", "lon"), check_vma=False
    )
```

```python
from functools import partial
import math

import jax
import jax.numpy as jnp
from jax import lax
from jax.sharding import PartitionSpec as P

radix_len = 64


def phase_table(row_total, col_total, modulus):
    product = (
        jnp.arange(row_total, dtype=jnp.int32)[:, None]
        * jnp.arange(col_total, dtype=jnp.int32)[None, :]
        % modulus
    )
    angle = product.astype(jnp.float32) * (2.0 * math.pi / modulus)
    return (jnp.cos(angle), jnp.sin(angle))


def filter_lines(lines, line_cut):
    line_total, circle = lines.shape
    outer = circle // radix_len
    mixer = partial(jnp.einsum, precision=lax.Precision.HIGH)
    outer_cos, outer_sin = phase_table(outer, outer, outer)
    inner_cos, inner_sin = phase_table(radix_len, radix_len, radix_len)
    twist_cos, twist_sin = phase_table(outer, radix_len, circle)
    values = lines.reshape(line_total, outer, radix_len)
    first_re = mixer("lan,aj->ljn", values, outer_cos)
    first_im = -mixer("lan,aj->ljn", values, outer_sin)
    turned_re = first_re * twist_cos + first_im * twist_sin
    turned_im = first_im * twist_cos - first_re * twist_sin
    spec_re = mixer("ljn,nk->ljk", turned_re, inner_cos) + mixer(
        "ljn,nk->ljk", turned_im, inner_sin
    )
    spec_im = mixer("ljn,nk->ljk", turned_im, inner_cos) - mixer(
        "ljn,nk->ljk", turned_re, inner_sin
    )
    wave = (
        jnp.arange(outer, dtype=jnp.int32)[:, None]
        + outer * jnp.arange(radix_len, dtype=jnp.int32)[None, :]
    )
    mode_value = jnp.minimum(wave, circle - wave).astype(jnp.float32)[None]
    cut_value = line_cut[:, None, None]
    damp = jnp.where(mode_value <= cut_value, 1.0, (cut_value / jnp.maximum(mode_value, 1.0)) ** 2)
    spec_re = spec_re * damp
    spec_im = spec_im * damp
    back_re = mixer("ljk,kn->ljn", spec_re, inner_cos) - mixer("ljk,kn->ljn", spec_im, inner_sin)
    back_im = mixer("ljk,kn->ljn", spec_im, inner_cos) + mixer("ljk,kn->ljn", spec_re, inner_sin)
    untwist_re = back_re * twist_cos - back_im * twist_sin
    untwist_im = back_im * twist_cos + back_re * twist_sin
    result = mixer("ljn,ja->lan", untwist_re, outer_cos) - mixer(
        "ljn,ja->lan", untwist_im, outer_sin
    )
    return (result / circle).reshape(line_total, circle)


def face_flux(courant, near_value, far_value):
    return 0.5 * courant * (near_value + far_value) - 0.5 * courant * courant * (
        far_value - near_value
    )


def body(fields, lon_courant, lat_courant, filter_rows, cutoff):
    field_count, level_count, rows_dev, columns = fields.shape
    stacked = field_count * level_count
    lon_devices = lax.axis_size("lon")
    lat_devices = lax.axis_size("lat")
    flat_fields = fields.reshape(stacked, rows_dev, columns)
    eastward = [(i, (i + 1) % lon_devices) for i in range(lon_devices)]
    westward = [((i + 1) % lon_devices, i) for i in range(lon_devices)]
    northward = [(i, i + 1) for i in range(lat_devices - 1)]
    southward = [(i + 1, i) for i in range(lat_devices - 1)]
    from_west = lax.ppermute(
        jnp.concatenate([flat_fields[..., -1], lon_courant[..., -1]], axis=0), "lon", eastward
    )
    from_east = lax.ppermute(flat_fields[..., 0], "lon", westward)
    from_below = lax.ppermute(
        jnp.concatenate([flat_fields[:, -1], lat_courant[:, -1]], axis=0), "lat", northward
    )
    from_above = lax.ppermute(flat_fields[:, 0], "lat", southward)
    wide_fields = jnp.concatenate(
        [from_west[:stacked, :, None], flat_fields, from_east[:, :, None]], axis=2
    ).reshape(field_count, level_count, rows_dev, columns + 2)
    wide_courant = jnp.concatenate([from_west[stacked:, :, None], lon_courant], axis=2)
    column_flux = face_flux(wide_courant, wide_fields[..., :-1], wide_fields[..., 1:])
    tall_fields = jnp.concatenate(
        [from_below[:stacked, None], flat_fields, from_above[:, None]], axis=1
    ).reshape(field_count, level_count, rows_dev + 2, columns)
    tall_courant = jnp.concatenate([from_below[stacked:, None], lat_courant], axis=1)
    row_flux = face_flux(tall_courant, tall_fields[:, :, :-1], tall_fields[:, :, 1:])
    tile_index = lax.axis_index("lat")
    lower_row = tile_index * rows_dev - 1 + jnp.arange(rows_dev + 1, dtype=jnp.int32)
    row_flux = jnp.where((lower_row == rows_dev * lat_devices - 1)[:, None], 0.0, row_flux)
    increment = -(column_flux[..., 1:] - column_flux[..., :-1]) - (
        row_flux[:, :, 1:] - row_flux[:, :, :-1]
    )
    flat_increment = increment.reshape(stacked, rows_dev, columns)
    half_rows = rows_dev // 2
    pair_shift = lat_devices // 2
    pair_perm = [(i, (i + pair_shift) % lat_devices) for i in range(lat_devices)]
    is_low = tile_index < pair_shift
    partner_index = (tile_index + pair_shift) % lat_devices

    def row_info(tile):
        row_global = tile * rows_dev + jnp.arange(rows_dev, dtype=jnp.int32)
        matched = filter_rows[None, :] == row_global[:, None]
        return jnp.any(matched, axis=1), jnp.sum(jnp.where(matched, cutoff[None, :], 0), axis=1)

    is_filtered, own_cut = row_info(tile_index)
    _, partner_cut = row_info(partner_index)
    row_cut = jnp.where(is_filtered, own_cut, partner_cut).astype(jnp.float32)
    low_half = flat_increment[:, :half_rows]
    high_half = flat_increment[:, half_rows:]
    kept = jnp.where(is_low, low_half, high_half)
    given = jnp.where(is_low, high_half, low_half)
    kept_filtered = jnp.where(is_low, is_filtered[:half_rows], is_filtered[half_rows:])
    kept_cut = jnp.where(is_low, row_cut[:half_rows], row_cut[half_rows:])
    chunk_sizes = (stacked * 2 // 5, stacked - stacked * 2 // 5)
    returned_parts, handed_parts = [], []
    chunk_start = 0
    for chunk_stack in chunk_sizes:
        rows_of_part = slice(chunk_start, chunk_start + chunk_stack)
        chunk_start += chunk_stack
        line_count = chunk_stack * half_rows // lon_devices
        line_index = lax.axis_index("lon") * line_count + jnp.arange(line_count, dtype=jnp.int32)
        line_cut = kept_cut[line_index % half_rows]
        taken = lax.ppermute(given[rows_of_part], "lat", pair_perm)
        pair_lines = jnp.where(kept_filtered[None, :, None], kept[rows_of_part], taken)
        full_lines = lax.all_to_all(
            pair_lines.reshape(chunk_stack * half_rows, columns),
            "lon",
            split_axis=0,
            concat_axis=1,
            tiled=True,
        )
        smoothed = filter_lines(full_lines, line_cut)
        returned = lax.all_to_all(
            smoothed, "lon", split_axis=1, concat_axis=0, tiled=True
        ).reshape(chunk_stack, half_rows, columns)
        returned_parts.append(returned)
        handed_parts.append(lax.ppermute(returned, "lat", pair_perm))
    returned = jnp.concatenate(returned_parts, axis=0)
    handed_back = jnp.concatenate(handed_parts, axis=0)
    smooth_rows = jnp.where(
        is_low,
        jnp.concatenate([returned, handed_back], axis=1),
        jnp.concatenate([handed_back, returned], axis=1),
    )
    final_increment = jnp.where(is_filtered[None, :, None], smooth_rows, flat_increment)
    return (flat_fields + final_increment).reshape(fields.shape)


def solution(mesh):
    placed = (P(None, None, "lat", "lon"), P(None, "lat", "lon"), P(None, "lat", "lon"), P(), P())
    return jax.shard_map(
        body, mesh=mesh, in_specs=placed, out_specs=P(None, None, "lat", "lon"), check_vma=False
    )
```
